256 devices in a mesh: pipe: 4 (over y_lo, core), seq: 64 (over y_hi, z, x).
Axes of the slice: x: 4, y: 4 (y_hi: 2, y_lo: 2; y = y_hi * 2 + y_lo), z: 8, core: 2. Of those that a mesh axis runs over, the one named last changes fastest.
Arguments:
- query_act: bfloat16 [4, 24576, 2048], P('pipe', 'seq'), may hold values from -6 to 6
- key_act: bfloat16 [4, 24576, 2048], P('pipe', 'seq'), may hold values from -6 to 6
- value_act: bfloat16 [4, 24576, 2048], P('pipe', 'seq'), may hold values from -6 to 6
- out_grad: bfloat16 [4, 24576, 2048], P('pipe', 'seq'), may hold values from -6 to 6
- local_lists: int32 [192, 5], P('seq'), may hold values from 0 to 191, as said below
- strided_lists: int32 [192, 2], P('seq'), may hold values from 0 to 191, as said below
Outputs:
- handed_query: bfloat16 [4, 24576, 2048], P('pipe', 'seq')
- handed_key: bfloat16 [4, 24576, 2048], P('pipe', 'seq')
- handed_value: bfloat16 [4, 24576, 2048], P('pipe', 'seq')
The draws below stay inside these ranges and needn't reach their ends.
Inputs may be any that keep to these rules, and one draw needn't show every extreme that they name: `local_lists`: each list names the query block itself, two different blocks 1 to 3 before it and two different blocks 1 to 3 after it, counted round the sequence. `strided_lists`: each list names the query block itself and one other block of the same aligned run of 3 blocks.
All inputs are finite; a program needn't handle non-finite values.
Results may differ from the reference program's by a relative error of at most 0.012.
Values may be sent and summed in bfloat16 or wider, within the bound.
No kernel may reach another device: no remote copies, remote signals or barrier semaphores. Data moves between devices by JAX's collectives and lax.ppermute only.
A program may use at most 192 MiB of HBM per device.

```python
import jax
import jax.numpy as jnp
from jax import lax

HEADS_ROW = 8
HEADS_COL = 8
HEAD_DIM = 128
BLOCK = 128
REACH = 3
LIST_ROW = 5
LIST_COL = 2
TOK_DEV = 384
SECTIONS = 4
SEQ = 24576
GROUPS = 64
GROUP_COLS = 16
ROWS = 24
BLOCKS = 192
FEAT = 2048


def shared_activations(key):
    subkeys = jax.random.split(jax.random.fold_in(key, 29), 2)
    shape = (SECTIONS, SEQ, FEAT)
    query_base = jnp.clip(jax.random.normal(subkeys[0], shape, jnp.float32), -4.0, 4.0)
    key_base = jnp.clip(jax.random.normal(subkeys[1], shape, jnp.float32), -4.0, 4.0)
    return (query_base, key_base)


def draw_query_act(key, part):
    return shared_activations(key)[0].astype(jnp.bfloat16)


def draw_key_act(key, part):
    return shared_activations(key)[1].astype(jnp.bfloat16)


def draw_local_lists(key, part):
    subkeys = jax.random.split(jax.random.fold_in(key, 41), 4)
    blocks = jnp.arange(BLOCKS, dtype=jnp.int32)
    first_back = jax.random.randint(subkeys[0], (BLOCKS,), 1, REACH + 1)
    second_back = (first_back - 1 + jax.random.randint(subkeys[1], (BLOCKS,), 1, REACH)) % REACH + 1
    first_ahead = jax.random.randint(subkeys[2], (BLOCKS,), 1, REACH + 1)
    second_ahead = (first_ahead - 1 + jax.random.randint(subkeys[3], (BLOCKS,), 1, REACH)) % REACH + 1
    entries = jnp.stack([blocks, blocks - first_back, blocks - second_back, blocks + first_ahead, blocks + second_ahead], axis=1) % BLOCKS
    return entries.astype(jnp.int32)


def draw_strided_lists(key, part):
    run_length = TOK_DEV // BLOCK
    blocks = jnp.arange(BLOCKS, dtype=jnp.int32)
    start = blocks - blocks % run_length
    other = start + (blocks % run_length + jax.random.randint(jax.random.fold_in(key, 53), (BLOCKS,), 1, run_length)) % run_length
    return jnp.stack([blocks, other], axis=1).astype(jnp.int32)


def block_levels(rng, extent, cuts, least, top_value):
    factor_of = 1.0
    for position, parts in cuts:
        heights = jax.random.uniform(jax.random.fold_in(jax.random.fold_in(rng, 6), position), (parts,), jnp.float32, least / len(cuts), top_value / len(cuts))
        factor_of = factor_of * jnp.repeat(jnp.exp(heights), extent[position] // parts).reshape((-1,) + (1,) * (len(extent) - 1 - position))
    return factor_of


def gaussian(key, dims, width, reach, cuts=(), kind=jnp.bfloat16):
    values = width * jax.random.normal(key, dims, jnp.float32)
    if cuts:
        values = values * block_levels(key, dims, cuts, -0.22, 0.18)
    return jnp.clip(values, -reach, reach).astype(kind)


def setup_inputs(seed: int = 0) -> dict:
    streams_of = jax.random.split(jax.random.key(seed), 7)
    query_act = draw_query_act(jax.random.fold_in(streams_of[6], 71), 0)
    key_act = draw_key_act(jax.random.fold_in(streams_of[6], 71), 0)
    value_act = gaussian(streams_of[2], (SECTIONS, SEQ, FEAT), 1.0, 6.0, ((0, 4), (1, 64)))
    out_grad = gaussian(streams_of[3], (SECTIONS, SEQ, FEAT), 1.0, 6.0, ((0, 4), (1, 64)))
    local_lists = draw_local_lists(jax.random.fold_in(streams_of[6], 71), 0)
    strided_lists = draw_strided_lists(jax.random.fold_in(streams_of[6], 71), 0)
    return dict(query_act=query_act, key_act=key_act, value_act=value_act, out_grad=out_grad, local_lists=local_lists, strided_lists=strided_lists)


def attend(query_blocks, key_list, value_list, grad_blocks):
    inverse_root = query_blocks.shape[-1] ** -0.5
    query_wide = query_blocks.astype(jnp.float32)
    key_wide = key_list.astype(jnp.float32)
    value_wide = value_list.astype(jnp.float32)
    grad_wide = grad_blocks.astype(jnp.float32)
    scores = jnp.einsum('nqd,nkd->nqk', query_wide, key_wide) * inverse_root
    largest = jnp.max(scores, axis=-1, keepdims=True)
    raised = jnp.exp(scores - largest)
    softmax = raised / jnp.sum(raised, axis=-1, keepdims=True)
    softmax_low = lax.optimization_barrier(softmax.astype(jnp.bfloat16)).astype(jnp.float32)
    attended = jnp.einsum('nqk,nkd->nqd', softmax_low, value_wide)
    row_delta = jnp.sum(grad_wide * attended, axis=-1, keepdims=True)
    grad_softmax = jnp.einsum('nqd,nkd->nqk', grad_wide, value_wide)
    grad_scores = lax.optimization_barrier((inverse_root * softmax * (grad_softmax - row_delta)).astype(jnp.bfloat16)).astype(jnp.float32)
    grad_query = jnp.einsum('nqk,nkd->nqd', grad_scores, key_wide)
    grad_klist = jnp.einsum('nqk,nqd->nkd', grad_scores, query_wide)
    grad_vlist = jnp.einsum('nqk,nqd->nkd', softmax_low, grad_wide)
    return grad_query, grad_klist, grad_vlist


def head_grads(query_part, key_part, value_part, grad_part, block_lists, head_count, list_count):
    def by_head(array):
        return array.reshape(BLOCKS, BLOCK, head_count, HEAD_DIM).transpose(2, 0, 1, 3)

    def per_head(pieces):
        query_head, key_head, value_head, grad_head = pieces
        key_list = key_head[block_lists].reshape(BLOCKS, list_count * BLOCK, HEAD_DIM)
        value_list = value_head[block_lists].reshape(BLOCKS, list_count * BLOCK, HEAD_DIM)
        grad_query, grad_klist, grad_vlist = attend(query_head, key_list, value_list, grad_head)
        grad_key = jnp.zeros((BLOCKS, BLOCK, HEAD_DIM), jnp.float32).at[block_lists].add(grad_klist.reshape(BLOCKS, list_count, BLOCK, HEAD_DIM))
        grad_value = jnp.zeros((BLOCKS, BLOCK, HEAD_DIM), jnp.float32).at[block_lists].add(grad_vlist.reshape(BLOCKS, list_count, BLOCK, HEAD_DIM))
        return grad_query, grad_key, grad_value

    results = lax.map(per_head, (by_head(query_part), by_head(key_part), by_head(value_part), by_head(grad_part)))
    return tuple(item.transpose(1, 2, 0, 3).reshape(SEQ, head_count * HEAD_DIM).astype(jnp.bfloat16) for item in results)


def to_columns(array):
    return array.reshape(ROWS, GROUP_COLS, GROUPS, array.shape[-1]).transpose(2, 1, 0, 3).reshape(SEQ, array.shape[-1])


def to_tokens(array):
    return array.reshape(GROUPS, GROUP_COLS, ROWS, array.shape[-1]).transpose(2, 1, 0, 3).reshape(SEQ, array.shape[-1])


def reference(query_act, key_act, value_act, out_grad, local_lists, strided_lists):
    row_width = HEADS_ROW * HEAD_DIM

    def one_section(pieces):
        query_now, key_now, value_now, grad_now = pieces
        row_side = head_grads(query_now[:, :row_width], key_now[:, :row_width], value_now[:, :row_width], grad_now[:, :row_width], local_lists, HEADS_ROW, LIST_ROW)
        column_side = head_grads(to_columns(query_now[:, row_width:]), to_columns(key_now[:, row_width:]), to_columns(value_now[:, row_width:]), to_columns(grad_now[:, row_width:]), strided_lists, HEADS_COL, LIST_COL)
        return tuple(jnp.concatenate([first, to_tokens(second)], axis=1) for first, second in zip(row_side, column_side))

    grads = lax.map(one_section, (query_act, key_act, value_act, out_grad))
    return (jnp.roll(grads[0], -1, axis=0), jnp.roll(grads[1], -1, axis=0), jnp.roll(grads[2], -1, axis=0))
```

```python
import jax
import jax.numpy as jnp
from jax import lax
from jax.experimental import pallas as pl
from jax.experimental.pallas import tpu as pltpu
from jax.sharding import PartitionSpec as P

HEADS_ROW = 8
HEADS_COL = 8
HEAD_DIM = 128
COLS = 1024
BLOCK = 128
REACH = 3
GROUP_COLS = 16


def shifted(value, axis, steps):
    count = lax.axis_size(axis)
    pairs = [(source, (source + steps) % count) for source in range(count)]
    return lax.ppermute(value, axis, pairs)


def chunk_grads(q, do, k, v, keep, scale):
    scores = lax.dot_general(q, k, (((1,), (1,)), ((), ())), preferred_element_type=jnp.float32)
    scores = jnp.where(keep, scores * scale, -jnp.inf)
    largest = jnp.max(scores, axis=1, keepdims=True)
    raised = jnp.exp(scores - largest)
    softmax = raised / jnp.sum(raised, axis=1, keepdims=True)
    softmax_low = softmax.astype(jnp.bfloat16)
    attended = jnp.dot(softmax_low, v, preferred_element_type=jnp.float32)
    row_delta = jnp.sum(do.astype(jnp.float32) * attended, axis=1, keepdims=True)
    grad_softmax = lax.dot_general(
        do, v, (((1,), (1,)), ((), ())), preferred_element_type=jnp.float32
    )
    grad_scores = (scale * softmax * (grad_softmax - row_delta)).astype(jnp.bfloat16)
    grad_q = jnp.dot(grad_scores, k, preferred_element_type=jnp.float32)
    grad_k = lax.dot_general(
        grad_scores, q, (((0,), (0,)), ((), ())), preferred_element_type=jnp.float32
    )
    grad_v = lax.dot_general(
        softmax_low, do, (((0,), (0,)), ((), ())), preferred_element_type=jnp.float32
    )
    return grad_q, grad_k, grad_v


def row_kernel(
    q_ref, do_ref, kp_ref, ko_ref, kn_ref, vp_ref, vo_ref, vn_ref, keep_ref,
    dq_ref, dprev_ref, down_ref, dnext_ref, kwin, vwin, dkwin, dvwin,
):
    tokens = q_ref.shape[0]
    span = (2 * REACH + 1) * BLOCK
    scale = HEAD_DIM ** (-0.5)
    kwin[0:tokens, :] = kp_ref[...]
    kwin[tokens:2 * tokens, :] = ko_ref[...]
    kwin[2 * tokens:3 * tokens, :] = kn_ref[...]
    vwin[0:tokens, :] = vp_ref[...]
    vwin[tokens:2 * tokens, :] = vo_ref[...]
    vwin[2 * tokens:3 * tokens, :] = vn_ref[...]
    dkwin[...] = jnp.zeros_like(dkwin)
    dvwin[...] = jnp.zeros_like(dvwin)
    for i in range(tokens // BLOCK):
        rows = slice(i * BLOCK, (i + 1) * BLOCK)
        keys = slice(i * BLOCK, i * BLOCK + span)
        keep = keep_ref[i:i + 1, :] > 0.5
        grad_q, grad_k, grad_v = chunk_grads(
            q_ref[rows, :], do_ref[rows, :], kwin[keys, :], vwin[keys, :], keep, scale
        )
        dq_ref[rows, :] = grad_q.astype(dq_ref.dtype)
        dkwin[keys, :] += grad_k
        dvwin[keys, :] += grad_v
    dprev_ref[0] = dkwin[0:tokens, :].astype(dprev_ref.dtype)
    dprev_ref[1] = dvwin[0:tokens, :].astype(dprev_ref.dtype)
    down_ref[0] = dkwin[tokens:2 * tokens, :]
    down_ref[1] = dvwin[tokens:2 * tokens, :]
    dnext_ref[0] = dkwin[2 * tokens:3 * tokens, :].astype(dnext_ref.dtype)
    dnext_ref[1] = dvwin[2 * tokens:3 * tokens, :].astype(dnext_ref.dtype)


def col_kernel(q_ref, k_ref, v_ref, do_ref, keep_ref, dq_ref, dk_ref, dv_ref):
    scale = HEAD_DIM ** (-0.5)
    keep = keep_ref[...] > 0.5
    grad_q, grad_k, grad_v = chunk_grads(
        q_ref[0], do_ref[0], k_ref[0], v_ref[0], keep, scale
    )
    dq_ref[0] = grad_q.astype(dq_ref.dtype)
    dk_ref[0] = grad_k.astype(dk_ref.dtype)
    dv_ref[0] = grad_v.astype(dv_ref.dtype)


def row_side(query_now, key_now, value_now, grad_now, near_before, near_after, keep):
    tokens = query_now.shape[0]
    span = (2 * REACH + 1) * BLOCK
    head_block = lambda h: (0, h)
    stacked_block = lambda part: pl.BlockSpec((None, tokens, HEAD_DIM), lambda h: (part, 0, h))
    plain = pl.BlockSpec((tokens, HEAD_DIM), head_block)
    pair_out = pl.BlockSpec((2, tokens, HEAD_DIM), lambda h: (0, 0, h))
    return pl.pallas_call(
        row_kernel,
        grid=(HEADS_ROW,),
        in_specs=[
            plain, plain,
            stacked_block(0), plain, stacked_block(0),
            stacked_block(1), plain, stacked_block(1),
            pl.BlockSpec(keep.shape, lambda h: (0, 0)),
        ],
        out_specs=[plain, pair_out, pair_out, pair_out],
        out_shape=[
            jax.ShapeDtypeStruct((tokens, HEADS_ROW * HEAD_DIM), jnp.bfloat16),
            jax.ShapeDtypeStruct((2, tokens, HEADS_ROW * HEAD_DIM), jnp.bfloat16),
            jax.ShapeDtypeStruct((2, tokens, HEADS_ROW * HEAD_DIM), jnp.float32),
            jax.ShapeDtypeStruct((2, tokens, HEADS_ROW * HEAD_DIM), jnp.bfloat16),
        ],
        scratch_shapes=[
            pltpu.VMEM((3 * tokens, HEAD_DIM), jnp.bfloat16),
            pltpu.VMEM((3 * tokens, HEAD_DIM), jnp.bfloat16),
            pltpu.VMEM((3 * tokens, HEAD_DIM), jnp.float32),
            pltpu.VMEM((3 * tokens, HEAD_DIM), jnp.float32),
        ],
    )(
        query_now, grad_now,
        near_before, key_now, near_after,
        near_before, value_now, near_after,
        keep,
    )


def col_side(received, keep):
    tokens = received.shape[1]
    part_block = lambda part: pl.BlockSpec((1, tokens, HEAD_DIM), lambda h: (part, 0, h))
    out_block = pl.BlockSpec((1, tokens, HEAD_DIM), lambda h: (0, 0, h))
    out_struct = jax.ShapeDtypeStruct((1, tokens, HEADS_COL * HEAD_DIM), jnp.bfloat16)
    return pl.pallas_call(
        col_kernel,
        grid=(HEADS_COL,),
        in_specs=[
            part_block(0), part_block(1), part_block(2), part_block(3),
            pl.BlockSpec(keep.shape, lambda h: (0, 0)),
        ],
        out_specs=[out_block, out_block, out_block],
        out_shape=[out_struct, out_struct, out_struct],
    )(received, received, received, received, keep)


def body(query_act, key_act, value_act, out_grad, local_lists, strided_lists):
    devices = lax.axis_size("seq")
    position = lax.axis_index("seq")
    query_now = query_act[0]
    key_now = key_act[0]
    value_now = value_act[0]
    grad_now = out_grad[0]
    tokens = query_now.shape[0]
    block_count = tokens // BLOCK
    total_blocks = block_count * devices
    row_width = HEADS_ROW * HEAD_DIM
    share = tokens // devices

    sent = jnp.stack([item[:, row_width:] for item in (query_now, key_now, value_now, grad_now)])
    received = lax.all_to_all(
        sent.reshape(4, share, devices, COLS), "seq", split_axis=2, concat_axis=1, tiled=True
    ).reshape(4, tokens, COLS)

    near = jnp.stack([key_now[:, :row_width], value_now[:, :row_width]])
    near_before = shifted(near, "seq", 1)
    near_after = shifted(near, "seq", -1)

    own_blocks = position * block_count + jnp.arange(block_count, dtype=jnp.int32)
    offsets = jnp.arange(-REACH, REACH + 1, dtype=jnp.int32)
    wanted = (own_blocks[:, None] + offsets[None, :]) % total_blocks
    row_allowed = jnp.any(wanted[:, :, None] == local_lists[:, None, :], axis=2)
    row_keep = jnp.repeat(row_allowed.astype(jnp.float32), BLOCK, axis=1)

    dq_row, d_prev, d_own, d_next = row_side(
        query_now, key_now, value_now, grad_now, near_before, near_after, row_keep
    )
    from_after = shifted(d_prev, "seq", -1).astype(jnp.float32)
    from_before = shifted(d_next, "seq", 1).astype(jnp.float32)
    d_total = (d_own + from_before + from_after).astype(jnp.bfloat16)
    row_grads = jnp.concatenate([dq_row[None], d_total], axis=0)
    row_handed = shifted(row_grads, "pipe", -1)

    grid_rows = tokens * devices // COLS
    arrival = jnp.arange(tokens, dtype=jnp.int32)
    col_block = ((arrival % GROUP_COLS) * grid_rows + arrival // GROUP_COLS) // BLOCK
    local_strided = strided_lists - position * block_count
    col_allowed = jnp.any(
        local_strided[:, None, :] == jnp.arange(block_count, dtype=jnp.int32)[None, :, None], axis=2
    )
    col_keep = col_allowed[col_block][:, col_block].astype(jnp.float32)
    col_grads = jnp.concatenate(col_side(received, col_keep), axis=0)
    returned = lax.all_to_all(
        col_grads.reshape(3, devices, share, 1, COLS), "seq", split_axis=1, concat_axis=3, tiled=True
    ).reshape(3, tokens, COLS)
    col_handed = shifted(returned, "pipe", -1)

    handed = jnp.concatenate([row_handed, col_handed], axis=2)
    return (handed[0][None], handed[1][None], handed[2][None])


def solution(mesh):
    in_specs = (
        P("pipe", "seq", None),
        P("pipe", "seq", None),
        P("pipe", "seq", None),
        P("pipe", "seq", None),
        P("seq", None),
        P("seq", None),
    )
    out_specs = (P("pipe", "seq", None), P("pipe", "seq", None), P("pipe", "seq", None))
    return jax.shard_map(body, mesh=mesh, in_specs=in_specs, out_specs=out_specs, check_vma=False)
```

```python
import jax
import jax.numpy as jnp
from jax import lax
from jax.experimental import pallas as pl
from jax.experimental.pallas import tpu as pltpu
from jax.sharding import PartitionSpec as P

HEADS_ROW = 8
HEADS_COL = 8
HEAD_DIM = 128
COLS = 1024
BLOCK = 128
REACH = 3
GROUP_COLS = 16


def shifted(value, axis, steps):
    count = lax.axis_size(axis)
    pairs = [(source, (source + steps) % count) for source in range(count)]
    return lax.ppermute(value, axis, pairs)


def chunk_grads(q, do, k, v, keep, scale):
    scores = lax.dot_general(q, k, (((1,), (1,)), ((), ())), preferred_element_type=jnp.float32)
    scores = jnp.where(keep, scores * scale, -jnp.inf)
    largest = jnp.max(scores, axis=1, keepdims=True)
    raised = jnp.exp(scores - largest)
    softmax = raised / jnp.sum(raised, axis=1, keepdims=True)
    softmax_low = softmax.astype(jnp.bfloat16)
    attended = jnp.dot(softmax_low, v, preferred_element_type=jnp.float32)
    row_delta = jnp.sum(do.astype(jnp.float32) * attended, axis=1, keepdims=True)
    grad_softmax = lax.dot_general(
        do, v, (((1,), (1,)), ((), ())), preferred_element_type=jnp.float32
    )
    grad_scores = (scale * softmax * (grad_softmax - row_delta)).astype(jnp.bfloat16)
    grad_q = jnp.dot(grad_scores, k, preferred_element_type=jnp.float32)
    grad_k = lax.dot_general(
        grad_scores, q, (((0,), (0,)), ((), ())), preferred_element_type=jnp.float32
    )
    grad_v = lax.dot_general(
        softmax_low, do, (((0,), (0,)), ((), ())), preferred_element_type=jnp.float32
    )
    return grad_q, grad_k, grad_v


def row_kernel(
    q_ref, do_ref, kp_ref, ko_ref, kn_ref, vp_ref, vo_ref, vn_ref, keep_ref,
    dq_ref, dprev_ref, down_ref, dnext_ref, kwin, vwin, dkwin, dvwin,
):
    tokens = q_ref.shape[0]
    span = (2 * REACH + 1) * BLOCK
    scale = HEAD_DIM ** (-0.5)
    kwin[0:tokens, :] = kp_ref[...]
    kwin[tokens:2 * tokens, :] = ko_ref[...]
    kwin[2 * tokens:3 * tokens, :] = kn_ref[...]
    vwin[0:tokens, :] = vp_ref[...]
    vwin[tokens:2 * tokens, :] = vo_ref[...]
    vwin[2 * tokens:3 * tokens, :] = vn_ref[...]
    dkwin[...] = jnp.zeros_like(dkwin)
    dvwin[...] = jnp.zeros_like(dvwin)
    for i in range(tokens // BLOCK):
        rows = slice(i * BLOCK, (i + 1) * BLOCK)
        keys = slice(i * BLOCK, i * BLOCK + span)
        keep = keep_ref[i:i + 1, :] > 0.5
        grad_q, grad_k, grad_v = chunk_grads(
            q_ref[rows, :], do_ref[rows, :], kwin[keys, :], vwin[keys, :], keep, scale
        )
        dq_ref[rows, :] = grad_q.astype(dq_ref.dtype)
        dkwin[keys, :] += grad_k
        dvwin[keys, :] += grad_v
    dprev_ref[0] = dkwin[0:tokens, :].astype(dprev_ref.dtype)
    dprev_ref[1] = dvwin[0:tokens, :].astype(dprev_ref.dtype)
    down_ref[0] = dkwin[tokens:2 * tokens, :]
    down_ref[1] = dvwin[tokens:2 * tokens, :]
    dnext_ref[0] = dkwin[2 * tokens:3 * tokens, :].astype(dnext_ref.dtype)
    dnext_ref[1] = dvwin[2 * tokens:3 * tokens, :].astype(dnext_ref.dtype)


def col_kernel(q_ref, k_ref, v_ref, do_ref, keep_ref, dq_ref, dk_ref, dv_ref):
    scale = HEAD_DIM ** (-0.5)
    keep = keep_ref[...] > 0.5
    grad_q, grad_k, grad_v = chunk_grads(
        q_ref[0], do_ref[0], k_ref[0], v_ref[0], keep, scale
    )
    dq_ref[0] = grad_q.astype(dq_ref.dtype)
    dk_ref[0] = grad_k.astype(dk_ref.dtype)
    dv_ref[0] = grad_v.astype(dv_ref.dtype)


def row_side(query_now, key_now, value_now, grad_now, near_before, near_after, keep):
    tokens = query_now.shape[0]
    span = (2 * REACH + 1) * BLOCK
    head_block = lambda h: (0, h)
    stacked_block = lambda part: pl.BlockSpec((None, tokens, HEAD_DIM), lambda h: (part, 0, h))
    plain = pl.BlockSpec((tokens, HEAD_DIM), head_block)
    pair_out = pl.BlockSpec((2, tokens, HEAD_DIM), lambda h: (0, 0, h))
    return pl.pallas_call(
        row_kernel,
        grid=(HEADS_ROW,),
        in_specs=[
            plain, plain,
            stacked_block(0), plain, stacked_block(0),
            stacked_block(1), plain, stacked_block(1),
            pl.BlockSpec(keep.shape, lambda h: (0, 0)),
        ],
        out_specs=[plain, pair_out, pair_out, pair_out],
        out_shape=[
            jax.ShapeDtypeStruct((tokens, HEADS_ROW * HEAD_DIM), jnp.bfloat16),
            jax.ShapeDtypeStruct((2, tokens, HEADS_ROW * HEAD_DIM), jnp.bfloat16),
            jax.ShapeDtypeStruct((2, tokens, HEADS_ROW * HEAD_DIM), jnp.float32),
            jax.ShapeDtypeStruct((2, tokens, HEADS_ROW * HEAD_DIM), jnp.bfloat16),
        ],
        scratch_shapes=[
            pltpu.VMEM((3 * tokens, HEAD_DIM), jnp.bfloat16),
            pltpu.VMEM((3 * tokens, HEAD_DIM), jnp.bfloat16),
            pltpu.VMEM((3 * tokens, HEAD_DIM), jnp.float32),
            pltpu.VMEM((3 * tokens, HEAD_DIM), jnp.float32),
        ],
    )(
        query_now, grad_now,
        near_before, key_now, near_after,
        near_before, value_now, near_after,
        keep,
    )


def col_side(received, keep):
    tokens = received.shape[1]
    part_block = lambda part: pl.BlockSpec((1, tokens, HEAD_DIM), lambda h: (part, 0, h))
    out_block = pl.BlockSpec((1, tokens, HEAD_DIM), lambda h: (0, 0, h))
    out_struct = jax.ShapeDtypeStruct((1, tokens, HEADS_COL * HEAD_DIM), jnp.bfloat16)
    return pl.pallas_call(
        col_kernel,
        grid=(HEADS_COL,),
        in_specs=[
            part_block(0), part_block(1), part_block(2), part_block(3),
            pl.BlockSpec(keep.shape, lambda h: (0, 0)),
        ],
        out_specs=[out_block, out_block, out_block],
        out_shape=[out_struct, out_struct, out_struct],
    )(received, received, received, received, keep)


def body(query_act, key_act, value_act, out_grad, local_lists, strided_lists):
    devices = lax.axis_size("seq")
    position = lax.axis_index("seq")
    query_now = query_act[0]
    key_now = key_act[0]
    value_now = value_act[0]
    grad_now = out_grad[0]
    tokens = query_now.shape[0]
    block_count = tokens // BLOCK
    total_blocks = block_count * devices
    row_width = HEADS_ROW * HEAD_DIM
    share = tokens // devices

    near = jnp.stack([key_now[:, :row_width], value_now[:, :row_width]])
    near_before = shifted(near, "seq", 1)
    near_after = shifted(near, "seq", -1)

    sent = jnp.stack([item[:, row_width:] for item in (query_now, key_now, value_now, grad_now)])
    sent, near_before, near_after = lax.optimization_barrier((sent, near_before, near_after))
    received = lax.all_to_all(
        sent.reshape(4, share, devices, COLS), "seq", split_axis=2, concat_axis=1, tiled=True
    ).reshape(4, tokens, COLS)

    own_blocks = position * block_count + jnp.arange(block_count, dtype=jnp.int32)
    offsets = jnp.arange(-REACH, REACH + 1, dtype=jnp.int32)
    wanted = (own_blocks[:, None] + offsets[None, :]) % total_blocks
    row_allowed = jnp.any(wanted[:, :, None] == local_lists[:, None, :], axis=2)
    row_keep = jnp.repeat(row_allowed.astype(jnp.float32), BLOCK, axis=1)

    dq_row, d_prev, d_own, d_next = row_side(
        query_now, key_now, value_now, grad_now, near_before, near_after, row_keep
    )
    from_after = shifted(d_prev, "seq", -1).astype(jnp.float32)
    from_before = shifted(d_next, "seq", 1).astype(jnp.float32)
    d_total = (d_own + from_before + from_after).astype(jnp.bfloat16)
    row_grads = jnp.concatenate([dq_row[None], d_total], axis=0)
    row_handed = shifted(row_grads, "pipe", -1)

    grid_rows = tokens * devices // COLS
    arrival = jnp.arange(tokens, dtype=jnp.int32)
    col_block = ((arrival % GROUP_COLS) * grid_rows + arrival // GROUP_COLS) // BLOCK
    local_strided = strided_lists - position * block_count
    col_allowed = jnp.any(
        local_strided[:, None, :] == jnp.arange(block_count, dtype=jnp.int32)[None, :, None], axis=2
    )
    col_keep = col_allowed[col_block][:, col_block].astype(jnp.float32)
    col_grads = jnp.concatenate(col_side(received, col_keep), axis=0)
    returned = lax.all_to_all(
        col_grads.reshape(3, devices, share, 1, COLS), "seq", split_axis=1, concat_axis=3, tiled=True
    ).reshape(3, tokens, COLS)
    col_handed = shifted(returned, "pipe", -1)

    handed = jnp.concatenate([row_handed, col_handed], axis=2)
    return (handed[0][None], handed[1][None], handed[2][None])


def solution(mesh):
    in_specs = (
        P("pipe", "seq", None),
        P("pipe", "seq", None),
        P("pipe", "seq", None),
        P("pipe", "seq", None),
        P("seq", None),
        P("seq", None),
    )
    out_specs = (P("pipe", "seq", None), P("pipe", "seq", None), P("pipe", "seq", None))
    return jax.shard_map(body, mesh=mesh, in_specs=in_specs, out_specs=out_specs, check_vma=False)
```

```python
import jax
import jax.numpy as jnp
from jax import lax
from jax.experimental import pallas as pl
from jax.experimental.pallas import tpu as pltpu
from jax.sharding import PartitionSpec as P

HEADS_ROW = 8
HEADS_COL = 8
HEAD_DIM = 128
COLS = 1024
BLOCK = 128
REACH = 3
GROUP_COLS = 16


def shifted(value, axis, steps):
    count = lax.axis_size(axis)
    pairs = [(source, (source + steps) % count) for source in range(count)]
    return lax.ppermute(value, axis, pairs)


def chunk_grads(q, do, k, v, keep, scale):
    scores = lax.dot_general(q, k, (((1,), (1,)), ((), ())), preferred_element_type=jnp.float32)
    scores = jnp.where(keep, scores * scale, -jnp.inf)
    largest = jnp.max(scores, axis=1, keepdims=True)
    raised = jnp.exp(scores - largest)
    softmax = raised / jnp.sum(raised, axis=1, keepdims=True)
    softmax_low = softmax.astype(jnp.bfloat16)
    attended = jnp.dot(softmax_low, v, preferred_element_type=jnp.float32)
    row_delta = jnp.sum(do.astype(jnp.float32) * attended, axis=1, keepdims=True)
    grad_softmax = lax.dot_general(
        do, v, (((1,), (1,)), ((), ())), preferred_element_type=jnp.float32
    )
    grad_scores = (scale * softmax * (grad_softmax - row_delta)).astype(jnp.bfloat16)
    grad_q = jnp.dot(grad_scores, k, preferred_element_type=jnp.float32)
    grad_k = lax.dot_general(
        grad_scores, q, (((0,), (0,)), ((), ())), preferred_element_type=jnp.float32
    )
    grad_v = lax.dot_general(
        softmax_low, do, (((0,), (0,)), ((), ())), preferred_element_type=jnp.float32
    )
    return grad_q, grad_k, grad_v


def row_kernel(
    q_ref, do_ref, kp_ref, ko_ref, kn_ref, vp_ref, vo_ref, vn_ref, keep_ref,
    dq_ref, dprev_ref, down_ref, dnext_ref, kwin, vwin, dkwin, dvwin,
):
    tokens = q_ref.shape[0]
    span = (2 * REACH + 1) * BLOCK
    scale = HEAD_DIM ** (-0.5)
    kwin[0:tokens, :] = kp_ref[...]
    kwin[tokens:2 * tokens, :] = ko_ref[...]
    kwin[2 * tokens:3 * tokens, :] = kn_ref[...]
    vwin[0:tokens, :] = vp_ref[...]
    vwin[tokens:2 * tokens, :] = vo_ref[...]
    vwin[2 * tokens:3 * tokens, :] = vn_ref[...]
    dkwin[...] = jnp.zeros_like(dkwin)
    dvwin[...] = jnp.zeros_like(dvwin)
    for i in range(tokens // BLOCK):
        rows = slice(i * BLOCK, (i + 1) * BLOCK)
        keys = slice(i * BLOCK, i * BLOCK + span)
        keep = keep_ref[i:i + 1, :] > 0.5
        grad_q, grad_k, grad_v = chunk_grads(
            q_ref[rows, :], do_ref[rows, :], kwin[keys, :], vwin[keys, :], keep, scale
        )
        dq_ref[rows, :] = grad_q.astype(dq_ref.dtype)
        dkwin[keys, :] += grad_k
        dvwin[keys, :] += grad_v
    dprev_ref[0] = dkwin[0:tokens, :].astype(dprev_ref.dtype)
    dprev_ref[1] = dvwin[0:tokens, :].astype(dprev_ref.dtype)
    down_ref[0] = dkwin[tokens:2 * tokens, :]
    down_ref[1] = dvwin[tokens:2 * tokens, :]
    dnext_ref[0] = dkwin[2 * tokens:3 * tokens, :].astype(dnext_ref.dtype)
    dnext_ref[1] = dvwin[2 * tokens:3 * tokens, :].astype(dnext_ref.dtype)


def col_kernel(q_ref, k_ref, v_ref, do_ref, keep_ref, dq_ref, dk_ref, dv_ref):
    scale = HEAD_DIM ** (-0.5)
    keep = keep_ref[...] > 0.5
    grad_q, grad_k, grad_v = chunk_grads(
        q_ref[0], do_ref[0], k_ref[0], v_ref[0], keep, scale
    )
    dq_ref[0] = grad_q.astype(dq_ref.dtype)
    dk_ref[0] = grad_k.astype(dk_ref.dtype)
    dv_ref[0] = grad_v.astype(dv_ref.dtype)


def row_side(query_now, key_now, value_now, grad_now, near_before, near_after, keep):
    tokens = query_now.shape[0]
    span = (2 * REACH + 1) * BLOCK
    head_block = lambda h: (0, h)
    stacked_block = lambda part: pl.BlockSpec((None, tokens, HEAD_DIM), lambda h: (part, 0, h))
    plain = pl.BlockSpec((tokens, HEAD_DIM), head_block)
    pair_out = pl.BlockSpec((2, tokens, HEAD_DIM), lambda h: (0, 0, h))
    return pl.pallas_call(
        row_kernel,
        grid=(HEADS_ROW,),
        in_specs=[
            plain, plain,
            stacked_block(0), plain, stacked_block(0),
            stacked_block(1), plain, stacked_block(1),
            pl.BlockSpec(keep.shape, lambda h: (0, 0)),
        ],
        out_specs=[plain, pair_out, pair_out, pair_out],
        out_shape=[
            jax.ShapeDtypeStruct((tokens, HEADS_ROW * HEAD_DIM), jnp.bfloat16),
            jax.ShapeDtypeStruct((2, tokens, HEADS_ROW * HEAD_DIM), jnp.bfloat16),
            jax.ShapeDtypeStruct((2, tokens, HEADS_ROW * HEAD_DIM), jnp.float32),
            jax.ShapeDtypeStruct((2, tokens, HEADS_ROW * HEAD_DIM), jnp.bfloat16),
        ],
        scratch_shapes=[
            pltpu.VMEM((3 * tokens, HEAD_DIM), jnp.bfloat16),
            pltpu.VMEM((3 * tokens, HEAD_DIM), jnp.bfloat16),
            pltpu.VMEM((3 * tokens, HEAD_DIM), jnp.float32),
            pltpu.VMEM((3 * tokens, HEAD_DIM), jnp.float32),
        ],
    )(
        query_now, grad_now,
        near_before, key_now, near_after,
        near_before, value_now, near_after,
        keep,
    )


def col_side(received, keep):
    tokens = received.shape[1]
    part_block = lambda part: pl.BlockSpec((1, tokens, HEAD_DIM), lambda h: (part, 0, h))
    out_block = pl.BlockSpec((1, tokens, HEAD_DIM), lambda h: (0, 0, h))
    out_struct = jax.ShapeDtypeStruct((1, tokens, HEADS_COL * HEAD_DIM), jnp.bfloat16)
    return pl.pallas_call(
        col_kernel,
        grid=(HEADS_COL,),
        in_specs=[
            part_block(0), part_block(1), part_block(2), part_block(3),
            pl.BlockSpec(keep.shape, lambda h: (0, 0)),
        ],
        out_specs=[out_block, out_block, out_block],
        out_shape=[out_struct, out_struct, out_struct],
    )(received, received, received, received, keep)


def body(query_act, key_act, value_act, out_grad, local_lists, strided_lists):
    devices = lax.axis_size("seq")
    position = lax.axis_index("seq")
    query_now = query_act[0]
    key_now = key_act[0]
    value_now = value_act[0]
    grad_now = out_grad[0]
    tokens = query_now.shape[0]
    block_count = tokens // BLOCK
    total_blocks = block_count * devices
    row_width = HEADS_ROW * HEAD_DIM
    share = tokens // devices

    near = jnp.stack([key_now[:, :row_width], value_now[:, :row_width]])
    near_before = shifted(near, "seq", 1)
    near_after = shifted(near, "seq", -1)

    sent = jnp.stack([item[:, row_width:] for item in (query_now, key_now, value_now, grad_now)])
    sent, near_before, near_after = lax.optimization_barrier((sent, near_before, near_after))
    received = lax.all_to_all(
        sent.reshape(4, share, devices, COLS), "seq", split_axis=2, concat_axis=1, tiled=True
    ).reshape(4, tokens, COLS)

    own_blocks = position * block_count + jnp.arange(block_count, dtype=jnp.int32)
    offsets = jnp.arange(-REACH, REACH + 1, dtype=jnp.int32)
    wanted = (own_blocks[:, None] + offsets[None, :]) % total_blocks
    row_allowed = jnp.any(wanted[:, :, None] == local_lists[:, None, :], axis=2)
    row_keep = jnp.repeat(row_allowed.astype(jnp.float32), BLOCK, axis=1)

    dq_row, d_prev, d_own, d_next = row_side(
        query_now, key_now, value_now, grad_now, near_before, near_after, row_keep
    )
    from_after = shifted(d_prev, "seq", -1).astype(jnp.float32)
    from_before = shifted(d_next, "seq", 1).astype(jnp.float32)
    d_total = (d_own + from_before + from_after).astype(jnp.bfloat16)
    row_grads = jnp.concatenate([dq_row[None], d_total], axis=0)
    row_handed = shifted(row_grads, "pipe", -1)

    grid_rows = tokens * devices // COLS
    arrival = jnp.arange(tokens, dtype=jnp.int32)
    col_block = ((arrival % GROUP_COLS) * grid_rows + arrival // GROUP_COLS) // BLOCK
    local_strided = strided_lists - position * block_count
    col_allowed = jnp.any(
        local_strided[:, None, :] == jnp.arange(block_count, dtype=jnp.int32)[None, :, None], axis=2
    )
    col_keep = col_allowed[col_block][:, col_block].astype(jnp.float32)
    received, dq_row, d_prev, d_own, d_next = lax.optimization_barrier(
        (received, dq_row, d_prev, d_own, d_next)
    )
    col_grads = jnp.concatenate(col_side(received, col_keep), axis=0)
    returned = lax.all_to_all(
        col_grads.reshape(3, devices, share, 1, COLS), "seq", split_axis=1, concat_axis=3, tiled=True
    ).reshape(3, tokens, COLS)
    col_handed = shifted(returned, "pipe", -1)

    handed = jnp.concatenate([row_handed, col_handed], axis=2)
    return (handed[0][None], handed[1][None], handed[2][None])


def solution(mesh):
    in_specs = (
        P("pipe", "seq", None),
        P("pipe", "seq", None),
        P("pipe", "seq", None),
        P("pipe", "seq", None),
        P("seq", None),
        P("seq", None),
    )
    out_specs = (P("pipe", "seq", None), P("pipe", "seq", None), P("pipe", "seq", None))
    return jax.shard_map(body, mesh=mesh, in_specs=in_specs, out_specs=out_specs, check_vma=False)
```

```python
import jax
import jax.numpy as jnp
from jax import lax
from jax.experimental import pallas as pl
from jax.experimental.pallas import tpu as pltpu
from jax.sharding import PartitionSpec as P

HEADS_ROW = 8
HEADS_COL = 8
HEAD_DIM = 128
COLS = 1024
BLOCK = 128
REACH = 3
GROUP_COLS = 16


def shifted(value, axis, steps):
    count = lax.axis_size(axis)
    pairs = [(source, (source + steps) % count) for source in range(count)]
    return lax.ppermute(value, axis, pairs)


def chunk_grads(q, do, k, v, keep, scale):
    scores = lax.dot_general(q, k, (((1,), (1,)), ((), ())), preferred_element_type=jnp.float32)
    scores = jnp.where(keep, scores * scale, -jnp.inf)
    largest = jnp.max(scores, axis=1, keepdims=True)
    raised = jnp.exp(scores - largest)
    softmax = raised / jnp.sum(raised, axis=1, keepdims=True)
    softmax_low = softmax.astype(jnp.bfloat16)
    attended = jnp.dot(softmax_low, v, preferred_element_type=jnp.float32)
    row_delta = jnp.sum(do.astype(jnp.float32) * attended, axis=1, keepdims=True)
    grad_softmax = lax.dot_general(
        do, v, (((1,), (1,)), ((), ())), preferred_element_type=jnp.float32
    )
    grad_scores = (scale * softmax * (grad_softmax - row_delta)).astype(jnp.bfloat16)
    grad_q = jnp.dot(grad_scores, k, preferred_element_type=jnp.float32)
    grad_k = lax.dot_general(
        grad_scores, q, (((0,), (0,)), ((), ())), preferred_element_type=jnp.float32
    )
    grad_v = lax.dot_general(
        softmax_low, do, (((0,), (0,)), ((), ())), preferred_element_type=jnp.float32
    )
    return grad_q, grad_k, grad_v


def row_kernel(
    q_ref, do_ref, kp_ref, ko_ref, kn_ref, vp_ref, vo_ref, vn_ref, keep_ref,
    dq_ref, dprev_ref, down_ref, dnext_ref, kwin, vwin, dkwin, dvwin,
):
    tokens = q_ref.shape[0]
    span = (2 * REACH + 1) * BLOCK
    scale = HEAD_DIM ** (-0.5)
    kwin[0:tokens, :] = kp_ref[...]
    kwin[tokens:2 * tokens, :] = ko_ref[...]
    kwin[2 * tokens:3 * tokens, :] = kn_ref[...]
    vwin[0:tokens, :] = vp_ref[...]
    vwin[tokens:2 * tokens, :] = vo_ref[...]
    vwin[2 * tokens:3 * tokens, :] = vn_ref[...]
    dkwin[...] = jnp.zeros_like(dkwin)
    dvwin[...] = jnp.zeros_like(dvwin)
    for i in range(tokens // BLOCK):
        rows = slice(i * BLOCK, (i + 1) * BLOCK)
        keys = slice(i * BLOCK, i * BLOCK + span)
        keep = keep_ref[i:i + 1, :] > 0.5
        grad_q, grad_k, grad_v = chunk_grads(
            q_ref[rows, :], do_ref[rows, :], kwin[keys, :], vwin[keys, :], keep, scale
        )
        dq_ref[rows, :] = grad_q.astype(dq_ref.dtype)
        dkwin[keys, :] += grad_k
        dvwin[keys, :] += grad_v
    dprev_ref[0] = dkwin[0:tokens, :].astype(dprev_ref.dtype)
    dprev_ref[1] = dvwin[0:tokens, :].astype(dprev_ref.dtype)
    down_ref[0] = dkwin[tokens:2 * tokens, :]
    down_ref[1] = dvwin[tokens:2 * tokens, :]
    dnext_ref[0] = dkwin[2 * tokens:3 * tokens, :].astype(dnext_ref.dtype)
    dnext_ref[1] = dvwin[2 * tokens:3 * tokens, :].astype(dnext_ref.dtype)


def col_kernel(q_ref, k_ref, v_ref, do_ref, keep_ref, dq_ref, dk_ref, dv_ref):
    scale = HEAD_DIM ** (-0.5)
    keep = keep_ref[...] > 0.5
    grad_q, grad_k, grad_v = chunk_grads(
        q_ref[0], do_ref[0], k_ref[0], v_ref[0], keep, scale
    )
    dq_ref[0] = grad_q.astype(dq_ref.dtype)
    dk_ref[0] = grad_k.astype(dk_ref.dtype)
    dv_ref[0] = grad_v.astype(dv_ref.dtype)


def row_side(query_now, key_now, value_now, grad_now, near_before, near_after, keep):
    tokens = query_now.shape[0]
    span = (2 * REACH + 1) * BLOCK
    head_block = lambda h: (0, h)
    stacked_block = lambda part: pl.BlockSpec((None, tokens, HEAD_DIM), lambda h: (part, 0, h))
    plain = pl.BlockSpec((tokens, HEAD_DIM), head_block)
    pair_out = pl.BlockSpec((2, tokens, HEAD_DIM), lambda h: (0, 0, h))
    return pl.pallas_call(
        row_kernel,
        grid=(HEADS_ROW,),
        in_specs=[
            plain, plain,
            stacked_block(0), plain, stacked_block(0),
            stacked_block(1), plain, stacked_block(1),
            pl.BlockSpec(keep.shape, lambda h: (0, 0)),
        ],
        out_specs=[plain, pair_out, pair_out, pair_out],
        out_shape=[
            jax.ShapeDtypeStruct((tokens, HEADS_ROW * HEAD_DIM), jnp.bfloat16),
            jax.ShapeDtypeStruct((2, tokens, HEADS_ROW * HEAD_DIM), jnp.bfloat16),
            jax.ShapeDtypeStruct((2, tokens, HEADS_ROW * HEAD_DIM), jnp.float32),
            jax.ShapeDtypeStruct((2, tokens, HEADS_ROW * HEAD_DIM), jnp.bfloat16),
        ],
        scratch_shapes=[
            pltpu.VMEM((3 * tokens, HEAD_DIM), jnp.bfloat16),
            pltpu.VMEM((3 * tokens, HEAD_DIM), jnp.bfloat16),
            pltpu.VMEM((3 * tokens, HEAD_DIM), jnp.float32),
            pltpu.VMEM((3 * tokens, HEAD_DIM), jnp.float32),
        ],
    )(
        query_now, grad_now,
        near_before, key_now, near_after,
        near_before, value_now, near_after,
        keep,
    )


def col_side(received, keep):
    tokens = received.shape[1]
    part_block = lambda part: pl.BlockSpec((1, tokens, HEAD_DIM), lambda h: (part, 0, h))
    out_block = pl.BlockSpec((1, tokens, HEAD_DIM), lambda h: (0, 0, h))
    out_struct = jax.ShapeDtypeStruct((1, tokens, HEADS_COL * HEAD_DIM), jnp.bfloat16)
    return pl.pallas_call(
        col_kernel,
        grid=(HEADS_COL,),
        in_specs=[
            part_block(0), part_block(1), part_block(2), part_block(3),
            pl.BlockSpec(keep.shape, lambda h: (0, 0)),
        ],
        out_specs=[out_block, out_block, out_block],
        out_shape=[out_struct, out_struct, out_struct],
    )(received, received, received, received, keep)


def body(query_act, key_act, value_act, out_grad, local_lists, strided_lists):
    devices = lax.axis_size("seq")
    position = lax.axis_index("seq")
    query_now = query_act[0]
    key_now = key_act[0]
    value_now = value_act[0]
    grad_now = out_grad[0]
    tokens = query_now.shape[0]
    block_count = tokens // BLOCK
    total_blocks = block_count * devices
    row_width = HEADS_ROW * HEAD_DIM
    share = tokens // devices

    near = jnp.stack([key_now[:, :row_width], value_now[:, :row_width]])
    near_before = shifted(near, "seq", 1)
    near_after = shifted(near, "seq", -1)
    sent = jnp.stack([item[:, row_width:] for item in (query_now, key_now, value_now, grad_now)])
    sent = shifted(sent, "pipe", -1)

    sent, near_before, near_after = lax.optimization_barrier((sent, near_before, near_after))
    received = lax.all_to_all(
        sent.reshape(4, share, devices, COLS), "seq", split_axis=2, concat_axis=1, tiled=True
    ).reshape(4, tokens, COLS)

    own_blocks = position * block_count + jnp.arange(block_count, dtype=jnp.int32)
    offsets = jnp.arange(-REACH, REACH + 1, dtype=jnp.int32)
    wanted = (own_blocks[:, None] + offsets[None, :]) % total_blocks
    row_allowed = jnp.any(wanted[:, :, None] == local_lists[:, None, :], axis=2)
    row_keep = jnp.repeat(row_allowed.astype(jnp.float32), BLOCK, axis=1)

    dq_row, d_prev, d_own, d_next = row_side(
        query_now, key_now, value_now, grad_now, near_before, near_after, row_keep
    )

    received, dq_row, d_prev, d_own, d_next = lax.optimization_barrier(
        (received, dq_row, d_prev, d_own, d_next)
    )
    from_after = shifted(d_prev, "seq", -1)
    from_before = shifted(d_next, "seq", 1)

    grid_rows = tokens * devices // COLS
    arrival = jnp.arange(tokens, dtype=jnp.int32)
    col_block = ((arrival % GROUP_COLS) * grid_rows + arrival // GROUP_COLS) // BLOCK
    local_strided = strided_lists - position * block_count
    col_allowed = jnp.any(
        local_strided[:, None, :] == jnp.arange(block_count, dtype=jnp.int32)[None, :, None], axis=2
    )
    col_keep = col_allowed[col_block][:, col_block].astype(jnp.float32)
    col_grads = jnp.concatenate(col_side(received, col_keep), axis=0)

    col_grads, from_after, from_before = lax.optimization_barrier((col_grads, from_after, from_before))
    d_total = (d_own + from_before.astype(jnp.float32) + from_after.astype(jnp.float32)).astype(
        jnp.bfloat16
    )
    row_grads = jnp.concatenate([dq_row[None], d_total], axis=0)
    row_handed = shifted(row_grads, "pipe", -1)
    col_handed = lax.all_to_all(
        col_grads.reshape(3, devices, share, 1, COLS), "seq", split_axis=1, concat_axis=3, tiled=True
    ).reshape(3, tokens, COLS)

    handed = jnp.concatenate([row_handed, col_handed], axis=2)
    return (handed[0][None], handed[1][None], handed[2][None])


def solution(mesh):
    in_specs = (
        P("pipe", "seq", None),
        P("pipe", "seq", None),
        P("pipe", "seq", None),
        P("pipe", "seq", None),
        P("seq", None),
        P("seq", None),
    )
    out_specs = (P("pipe", "seq", None), P("pipe", "seq", None), P("pipe", "seq", None))
    return jax.shard_map(body, mesh=mesh, in_specs=in_specs, out_specs=out_specs, check_vma=False)
```

```python
import jax
import jax.numpy as jnp
from jax import lax
from jax.experimental import pallas as pl
from jax.experimental.pallas import tpu as pltpu
from jax.sharding import PartitionSpec as P

HEADS_ROW = 8
HEADS_COL = 8
HEAD_DIM = 128
COLS = 1024
BLOCK = 128
REACH = 3
GROUP_COLS = 16


def shifted(value, axis, steps):
    count = lax.axis_size(axis)
    pairs = [(source, (source + steps) % count) for source in range(count)]
    return lax.ppermute(value, axis, pairs)


def chunk_grads(q, do, k, v, keep, scale):
    scores = lax.dot_general(q, k, (((1,), (1,)), ((), ())), preferred_element_type=jnp.float32)
    scores = jnp.where(keep, scores * scale, -jnp.inf)
    largest = jnp.max(scores, axis=1, keepdims=True)
    raised = jnp.exp(scores - largest)
    softmax = raised / jnp.sum(raised, axis=1, keepdims=True)
    softmax_low = softmax.astype(jnp.bfloat16)
    attended = jnp.dot(softmax_low, v, preferred_element_type=jnp.float32)
    row_delta = jnp.sum(do.astype(jnp.float32) * attended, axis=1, keepdims=True)
    grad_softmax = lax.dot_general(
        do, v, (((1,), (1,)), ((), ())), preferred_element_type=jnp.float32
    )
    grad_scores = (scale * softmax * (grad_softmax - row_delta)).astype(jnp.bfloat16)
    grad_q = jnp.dot(grad_scores, k, preferred_element_type=jnp.float32)
    grad_k = lax.dot_general(
        grad_scores, q, (((0,), (0,)), ((), ())), preferred_element_type=jnp.float32
    )
    grad_v = lax.dot_general(
        softmax_low, do, (((0,), (0,)), ((), ())), preferred_element_type=jnp.float32
    )
    return grad_q, grad_k, grad_v


def row_kernel(
    q_ref, do_ref, kp_ref, ko_ref, kn_ref, vp_ref, vo_ref, vn_ref, keep_ref,
    dq_ref, dprev_ref, down_ref, dnext_ref, kwin, vwin, dkwin, dvwin,
):
    tokens = q_ref.shape[0]
    span = (2 * REACH + 1) * BLOCK
    scale = HEAD_DIM ** (-0.5)
    kwin[0:tokens, :] = kp_ref[...]
    kwin[tokens:2 * tokens, :] = ko_ref[...]
    kwin[2 * tokens:3 * tokens, :] = kn_ref[...]
    vwin[0:tokens, :] = vp_ref[...]
    vwin[tokens:2 * tokens, :] = vo_ref[...]
    vwin[2 * tokens:3 * tokens, :] = vn_ref[...]
    dkwin[...] = jnp.zeros_like(dkwin)
    dvwin[...] = jnp.zeros_like(dvwin)
    for i in range(tokens // BLOCK):
        rows = slice(i * BLOCK, (i + 1) * BLOCK)
        keys = slice(i * BLOCK, i * BLOCK + span)
        keep = keep_ref[i:i + 1, :] > 0.5
        grad_q, grad_k, grad_v = chunk_grads(
            q_ref[rows, :], do_ref[rows, :], kwin[keys, :], vwin[keys, :], keep, scale
        )
        dq_ref[rows, :] = grad_q.astype(dq_ref.dtype)
        dkwin[keys, :] += grad_k
        dvwin[keys, :] += grad_v
    dprev_ref[0] = dkwin[0:tokens, :].astype(dprev_ref.dtype)
    dprev_ref[1] = dvwin[0:tokens, :].astype(dprev_ref.dtype)
    down_ref[0] = dkwin[tokens:2 * tokens, :]
    down_ref[1] = dvwin[tokens:2 * tokens, :]
    dnext_ref[0] = dkwin[2 * tokens:3 * tokens, :].astype(dnext_ref.dtype)
    dnext_ref[1] = dvwin[2 * tokens:3 * tokens, :].astype(dnext_ref.dtype)


def col_kernel(q_ref, k_ref, v_ref, do_ref, keep_ref, dq_ref, dk_ref, dv_ref):
    scale = HEAD_DIM ** (-0.5)
    keep = keep_ref[...] > 0.5
    grad_q, grad_k, grad_v = chunk_grads(
        q_ref[0], do_ref[0], k_ref[0], v_ref[0], keep, scale
    )
    dq_ref[0] = grad_q.astype(dq_ref.dtype)
    dk_ref[0] = grad_k.astype(dk_ref.dtype)
    dv_ref[0] = grad_v.astype(dv_ref.dtype)


def row_side(query_now, key_now, value_now, grad_now, near_before, near_after, keep):
    tokens = query_now.shape[0]
    span = (2 * REACH + 1) * BLOCK
    head_block = lambda h: (0, h)
    stacked_block = lambda part: pl.BlockSpec((None, tokens, HEAD_DIM), lambda h: (part, 0, h))
    plain = pl.BlockSpec((tokens, HEAD_DIM), head_block)
    pair_out = pl.BlockSpec((2, tokens, HEAD_DIM), lambda h: (0, 0, h))
    return pl.pallas_call(
        row_kernel,
        grid=(HEADS_ROW,),
        in_specs=[
            plain, plain,
            stacked_block(0), plain, stacked_block(0),
            stacked_block(1), plain, stacked_block(1),
            pl.BlockSpec(keep.shape, lambda h: (0, 0)),
        ],
        out_specs=[plain, pair_out, pair_out, pair_out],
        out_shape=[
            jax.ShapeDtypeStruct((tokens, HEADS_ROW * HEAD_DIM), jnp.bfloat16),
            jax.ShapeDtypeStruct((2, tokens, HEADS_ROW * HEAD_DIM), jnp.bfloat16),
            jax.ShapeDtypeStruct((2, tokens, HEADS_ROW * HEAD_DIM), jnp.float32),
            jax.ShapeDtypeStruct((2, tokens, HEADS_ROW * HEAD_DIM), jnp.bfloat16),
        ],
        scratch_shapes=[
            pltpu.VMEM((3 * tokens, HEAD_DIM), jnp.bfloat16),
            pltpu.VMEM((3 * tokens, HEAD_DIM), jnp.bfloat16),
            pltpu.VMEM((3 * tokens, HEAD_DIM), jnp.float32),
            pltpu.VMEM((3 * tokens, HEAD_DIM), jnp.float32),
        ],
    )(
        query_now, grad_now,
        near_before, key_now, near_after,
        near_before, value_now, near_after,
        keep,
    )


def col_side(received, keep):
    tokens = received.shape[1]
    part_block = lambda part: pl.BlockSpec((1, tokens, HEAD_DIM), lambda h: (part, 0, h))
    out_block = pl.BlockSpec((1, tokens, HEAD_DIM), lambda h: (0, 0, h))
    out_struct = jax.ShapeDtypeStruct((1, tokens, HEADS_COL * HEAD_DIM), jnp.bfloat16)
    return pl.pallas_call(
        col_kernel,
        grid=(HEADS_COL,),
        in_specs=[
            part_block(0), part_block(1), part_block(2), part_block(3),
            pl.BlockSpec(keep.shape, lambda h: (0, 0)),
        ],
        out_specs=[out_block, out_block, out_block],
        out_shape=[out_struct, out_struct, out_struct],
    )(received, received, received, received, keep)


def body(query_act, key_act, value_act, out_grad, local_lists, strided_lists):
    devices = lax.axis_size("seq")
    position = lax.axis_index("seq")
    query_now = query_act[0]
    key_now = key_act[0]
    value_now = value_act[0]
    grad_now = out_grad[0]
    tokens = query_now.shape[0]
    block_count = tokens // BLOCK
    total_blocks = block_count * devices
    row_width = HEADS_ROW * HEAD_DIM
    share = tokens // devices

    sent = jnp.stack([item[:, row_width:] for item in (query_now, key_now, value_now, grad_now)])
    received = lax.all_to_all(
        sent.reshape(4, share, devices, COLS), "seq", split_axis=2, concat_axis=1, tiled=True
    ).reshape(4, tokens, COLS)

    near = jnp.stack([key_now[:, :row_width], value_now[:, :row_width]])
    near_before = shifted(near, "seq", 1)
    near_after = shifted(near, "seq", -1)

    own_blocks = position * block_count + jnp.arange(block_count, dtype=jnp.int32)
    offsets = jnp.arange(-REACH, REACH + 1, dtype=jnp.int32)
    wanted = (own_blocks[:, None] + offsets[None, :]) % total_blocks
    row_allowed = jnp.any(wanted[:, :, None] == local_lists[:, None, :], axis=2)
    row_keep = jnp.repeat(row_allowed.astype(jnp.float32), BLOCK, axis=1)

    dq_row, d_prev, d_own, d_next = row_side(
        query_now, key_now, value_now, grad_now, near_before, near_after, row_keep
    )
    from_after = shifted(d_prev, "seq", -1)
    from_before = shifted(d_next, "seq", 1)

    received, from_after, from_before = lax.optimization_barrier((received, from_after, from_before))

    grid_rows = tokens * devices // COLS
    arrival = jnp.arange(tokens, dtype=jnp.int32)
    col_block = ((arrival % GROUP_COLS) * grid_rows + arrival // GROUP_COLS) // BLOCK
    local_strided = strided_lists - position * block_count
    col_allowed = jnp.any(
        local_strided[:, None, :] == jnp.arange(block_count, dtype=jnp.int32)[None, :, None], axis=2
    )
    col_keep = col_allowed[col_block][:, col_block].astype(jnp.float32)
    col_grads = jnp.concatenate(col_side(received, col_keep), axis=0)

    d_total = (d_own + from_before.astype(jnp.float32) + from_after.astype(jnp.float32)).astype(
        jnp.bfloat16
    )
    row_grads = jnp.concatenate([dq_row[None], d_total], axis=0)
    row_handed = shifted(row_grads, "pipe", -1)
    returned = lax.all_to_all(
        col_grads.reshape(3, devices, share, 1, COLS), "seq", split_axis=1, concat_axis=3, tiled=True
    ).reshape(3, tokens, COLS)
    col_handed = shifted(returned, "pipe", -1)

    handed = jnp.concatenate([row_handed, col_handed], axis=2)
    return (handed[0][None], handed[1][None], handed[2][None])


def solution(mesh):
    in_specs = (
        P("pipe", "seq", None),
        P("pipe", "seq", None),
        P("pipe", "seq", None),
        P("pipe", "seq", None),
        P("seq", None),
        P("seq", None),
    )
    out_specs = (P("pipe", "seq", None), P("pipe", "seq", None), P("pipe", "seq", None))
    return jax.shard_map(body, mesh=mesh, in_specs=in_specs, out_specs=out_specs, check_vma=False)
```

```python
import jax
import jax.numpy as jnp
from jax import lax
from jax.experimental import pallas as pl
from jax.experimental.pallas import tpu as pltpu
from jax.sharding import PartitionSpec as P

HEADS_ROW = 8
HEADS_COL = 8
HEAD_DIM = 128
COLS = 1024
BLOCK = 128
REACH = 3
GROUP_COLS = 16


def shifted(value, axis, steps):
    count = lax.axis_size(axis)
    pairs = [(source, (source + steps) % count) for source in range(count)]
    return lax.ppermute(value, axis, pairs)


def chunk_grads(q, do, k, v, keep, scale):
    scores = lax.dot_general(q, k, (((1,), (1,)), ((), ())), preferred_element_type=jnp.float32)
    scores = jnp.where(keep, scores * scale, -jnp.inf)
    largest = jnp.max(scores, axis=1, keepdims=True)
    raised = jnp.exp(scores - largest)
    softmax = raised / jnp.sum(raised, axis=1, keepdims=True)
    softmax_low = softmax.astype(jnp.bfloat16)
    attended = jnp.dot(softmax_low, v, preferred_element_type=jnp.float32)
    row_delta = jnp.sum(do.astype(jnp.float32) * attended, axis=1, keepdims=True)
    grad_softmax = lax.dot_general(
        do, v, (((1,), (1,)), ((), ())), preferred_element_type=jnp.float32
    )
    grad_scores = (scale * softmax * (grad_softmax - row_delta)).astype(jnp.bfloat16)
    grad_q = jnp.dot(grad_scores, k, preferred_element_type=jnp.float32)
    grad_k = lax.dot_general(
        grad_scores, q, (((0,), (0,)), ((), ())), preferred_element_type=jnp.float32
    )
    grad_v = lax.dot_general(
        softmax_low, do, (((0,), (0,)), ((), ())), preferred_element_type=jnp.float32
    )
    return grad_q, grad_k, grad_v


def row_kernel(
    q_ref, do_ref, kp_ref, ko_ref, kn_ref, vp_ref, vo_ref, vn_ref, keep_ref,
    dq_ref, dprev_ref, down_ref, dnext_ref, kwin, vwin, dkwin, dvwin,
):
    tokens = q_ref.shape[0]
    span = (2 * REACH + 1) * BLOCK
    scale = HEAD_DIM ** (-0.5)
    kwin[0:tokens, :] = kp_ref[...]
    kwin[tokens:2 * tokens, :] = ko_ref[...]
    kwin[2 * tokens:3 * tokens, :] = kn_ref[...]
    vwin[0:tokens, :] = vp_ref[...]
    vwin[tokens:2 * tokens, :] = vo_ref[...]
    vwin[2 * tokens:3 * tokens, :] = vn_ref[...]
    dkwin[...] = jnp.zeros_like(dkwin)
    dvwin[...] = jnp.zeros_like(dvwin)
    for i in range(tokens // BLOCK):
        rows = slice(i * BLOCK, (i + 1) * BLOCK)
        keys = slice(i * BLOCK, i * BLOCK + span)
        keep = keep_ref[i:i + 1, :] > 0.5
        grad_q, grad_k, grad_v = chunk_grads(
            q_ref[rows, :], do_ref[rows, :], kwin[keys, :], vwin[keys, :], keep, scale
        )
        dq_ref[rows, :] = grad_q.astype(dq_ref.dtype)
        dkwin[keys, :] += grad_k
        dvwin[keys, :] += grad_v
    dprev_ref[0] = dkwin[0:tokens, :].astype(dprev_ref.dtype)
    dprev_ref[1] = dvwin[0:tokens, :].astype(dprev_ref.dtype)
    down_ref[0] = dkwin[tokens:2 * tokens, :]
    down_ref[1] = dvwin[tokens:2 * tokens, :]
    dnext_ref[0] = dkwin[2 * tokens:3 * tokens, :].astype(dnext_ref.dtype)
    dnext_ref[1] = dvwin[2 * tokens:3 * tokens, :].astype(dnext_ref.dtype)


def col_kernel(q_ref, k_ref, v_ref, do_ref, keep_ref, out_ref):
    scale = HEAD_DIM ** (-0.5)
    keep = keep_ref[...] > 0.5
    grad_q, grad_k, grad_v = chunk_grads(
        q_ref[0], do_ref[0], k_ref[0], v_ref[0], keep, scale
    )
    out_ref[0] = grad_q.astype(out_ref.dtype)
    out_ref[1] = grad_k.astype(out_ref.dtype)
    out_ref[2] = grad_v.astype(out_ref.dtype)


def row_side(query_now, key_now, value_now, grad_now, near_before, near_after, keep):
    tokens = query_now.shape[0]
    span = (2 * REACH + 1) * BLOCK
    head_block = lambda h: (0, h)
    stacked_block = lambda part: pl.BlockSpec((None, tokens, HEAD_DIM), lambda h: (part, 0, h))
    plain = pl.BlockSpec((tokens, HEAD_DIM), head_block)
    pair_out = pl.BlockSpec((2, tokens, HEAD_DIM), lambda h: (0, 0, h))
    return pl.pallas_call(
        row_kernel,
        grid=(HEADS_ROW,),
        in_specs=[
            plain, plain,
            stacked_block(0), plain, stacked_block(0),
            stacked_block(1), plain, stacked_block(1),
            pl.BlockSpec(keep.shape, lambda h: (0, 0)),
        ],
        out_specs=[plain, pair_out, pair_out, pair_out],
        out_shape=[
            jax.ShapeDtypeStruct((tokens, HEADS_ROW * HEAD_DIM), jnp.bfloat16),
            jax.ShapeDtypeStruct((2, tokens, HEADS_ROW * HEAD_DIM), jnp.bfloat16),
            jax.ShapeDtypeStruct((2, tokens, HEADS_ROW * HEAD_DIM), jnp.float32),
            jax.ShapeDtypeStruct((2, tokens, HEADS_ROW * HEAD_DIM), jnp.bfloat16),
        ],
        scratch_shapes=[
            pltpu.VMEM((3 * tokens, HEAD_DIM), jnp.bfloat16),
            pltpu.VMEM((3 * tokens, HEAD_DIM), jnp.bfloat16),
            pltpu.VMEM((3 * tokens, HEAD_DIM), jnp.float32),
            pltpu.VMEM((3 * tokens, HEAD_DIM), jnp.float32),
        ],
    )(
        query_now, grad_now,
        near_before, key_now, near_after,
        near_before, value_now, near_after,
        keep,
    )


def col_side(received, keep):
    tokens = received.shape[1]
    part_block = lambda part: pl.BlockSpec((1, tokens, HEAD_DIM), lambda h: (part, 0, h))
    return pl.pallas_call(
        col_kernel,
        grid=(HEADS_COL,),
        in_specs=[
            part_block(0), part_block(1), part_block(2), part_block(3),
            pl.BlockSpec(keep.shape, lambda h: (0, 0)),
        ],
        out_specs=pl.BlockSpec((3, tokens, HEAD_DIM), lambda h: (0, 0, h)),
        out_shape=jax.ShapeDtypeStruct((3, tokens, HEADS_COL * HEAD_DIM), jnp.bfloat16),
    )(received, received, received, received, keep)


def body(query_act, key_act, value_act, out_grad, local_lists, strided_lists):
    devices = lax.axis_size("seq")
    position = lax.axis_index("seq")
    query_now = query_act[0]
    key_now = key_act[0]
    value_now = value_act[0]
    grad_now = out_grad[0]
    tokens = query_now.shape[0]
    block_count = tokens // BLOCK
    total_blocks = block_count * devices
    row_width = HEADS_ROW * HEAD_DIM
    share = tokens // devices

    near = jnp.stack([key_now[:, :row_width], value_now[:, :row_width]])
    near_before = shifted(near, "seq", 1)
    near_after = shifted(near, "seq", -1)
    sent = jnp.stack([item[:, row_width:] for item in (query_now, key_now, value_now, grad_now)])
    sent = shifted(sent, "pipe", -1)

    sent, near_before, near_after = lax.optimization_barrier((sent, near_before, near_after))
    received = lax.all_to_all(
        sent.reshape(4, share, devices, COLS), "seq", split_axis=2, concat_axis=1, tiled=True
    ).reshape(4, tokens, COLS)

    own_blocks = position * block_count + jnp.arange(block_count, dtype=jnp.int32)
    offsets = jnp.arange(-REACH, REACH + 1, dtype=jnp.int32)
    wanted = (own_blocks[:, None] + offsets[None, :]) % total_blocks
    row_allowed = jnp.any(wanted[:, :, None] == local_lists[:, None, :], axis=2)
    row_keep = jnp.repeat(row_allowed.astype(jnp.float32), BLOCK, axis=1)

    dq_row, d_prev, d_own, d_next = row_side(
        query_now, key_now, value_now, grad_now, near_before, near_after, row_keep
    )

    received, dq_row, d_prev, d_own, d_next = lax.optimization_barrier(
        (received, dq_row, d_prev, d_own, d_next)
    )
    from_after = shifted(d_prev, "seq", -1)
    from_before = shifted(d_next, "seq", 1)

    grid_rows = tokens * devices // COLS
    arrival = jnp.arange(tokens, dtype=jnp.int32)
    col_block = ((arrival % GROUP_COLS) * grid_rows + arrival // GROUP_COLS) // BLOCK
    local_strided = strided_lists - position * block_count
    listed = sum(
        (col_block == number)[:, None] * local_strided[number][None, :]
        for number in range(block_count)
    )
    col_keep = jnp.any(listed[:, :, None] == col_block[None, None, :], axis=1).astype(jnp.float32)
    col_grads = col_side(received, col_keep)

    col_grads, from_after, from_before = lax.optimization_barrier((col_grads, from_after, from_before))
    d_total = (d_own + from_before.astype(jnp.float32) + from_after.astype(jnp.float32)).astype(
        jnp.bfloat16
    )
    row_grads = jnp.concatenate([dq_row[None], d_total], axis=0)
    row_handed = shifted(row_grads, "pipe", -1)
    col_handed = lax.all_to_all(
        col_grads.reshape(3, devices, share, 1, COLS), "seq", split_axis=1, concat_axis=3, tiled=True
    ).reshape(3, tokens, COLS)

    handed = jnp.concatenate([row_handed, col_handed], axis=2)
    return (handed[0][None], handed[1][None], handed[2][None])


def solution(mesh):
    in_specs = (
        P("pipe", "seq", None),
        P("pipe", "seq", None),
        P("pipe", "seq", None),
        P("pipe", "seq", None),
        P("seq", None),
        P("seq", None),
    )
    out_specs = (P("pipe", "seq", None), P("pipe", "seq", None), P("pipe", "seq", None))
    return jax.shard_map(body, mesh=mesh, in_specs=in_specs, out_specs=out_specs, check_vma=False)
```

```python
import jax
import jax.numpy as jnp
from jax import lax
from jax.experimental import pallas as pl
from jax.experimental.pallas import tpu as pltpu
from jax.sharding import PartitionSpec as P

HEADS_ROW = 8
HEADS_COL = 8
HEAD_DIM = 128
COLS = 1024
BLOCK = 128
REACH = 3
GROUP_COLS = 16


def shifted(value, axis, steps):
    count = lax.axis_size(axis)
    pairs = [(source, (source + steps) % count) for source in range(count)]
    return lax.ppermute(value, axis, pairs)


def chunk_grads(q, do, k, v, keep, scale):
    scores = lax.dot_general(q, k, (((1,), (1,)), ((), ())), preferred_element_type=jnp.float32)
    scores = jnp.where(keep, scores * scale, -jnp.inf)
    largest = jnp.max(scores, axis=1, keepdims=True)
    raised = jnp.exp(scores - largest)
    softmax = raised / jnp.sum(raised, axis=1, keepdims=True)
    softmax_low = softmax.astype(jnp.bfloat16)
    attended = jnp.dot(softmax_low, v, preferred_element_type=jnp.float32)
    row_delta = jnp.sum(do.astype(jnp.float32) * attended, axis=1, keepdims=True)
    grad_softmax = lax.dot_general(
        do, v, (((1,), (1,)), ((), ())), preferred_element_type=jnp.float32
    )
    grad_scores = (scale * softmax * (grad_softmax - row_delta)).astype(jnp.bfloat16)
    grad_q = jnp.dot(grad_scores, k, preferred_element_type=jnp.float32)
    grad_k = lax.dot_general(
        grad_scores, q, (((0,), (0,)), ((), ())), preferred_element_type=jnp.float32
    )
    grad_v = lax.dot_general(
        softmax_low, do, (((0,), (0,)), ((), ())), preferred_element_type=jnp.float32
    )
    return grad_q, grad_k, grad_v


def row_kernel(
    q_ref, do_ref, kp_ref, ko_ref, kn_ref, vp_ref, vo_ref, vn_ref, keep_ref,
    dq_ref, dprev_ref, down_ref, dnext_ref, kwin, vwin, dkwin, dvwin,
):
    tokens = q_ref.shape[0]
    span = (2 * REACH + 1) * BLOCK
    scale = HEAD_DIM ** (-0.5)
    kwin[0:tokens, :] = kp_ref[...]
    kwin[tokens:2 * tokens, :] = ko_ref[...]
    kwin[2 * tokens:3 * tokens, :] = kn_ref[...]
    vwin[0:tokens, :] = vp_ref[...]
    vwin[tokens:2 * tokens, :] = vo_ref[...]
    vwin[2 * tokens:3 * tokens, :] = vn_ref[...]
    dkwin[...] = jnp.zeros_like(dkwin)
    dvwin[...] = jnp.zeros_like(dvwin)
    for i in range(tokens // BLOCK):
        rows = slice(i * BLOCK, (i + 1) * BLOCK)
        keys = slice(i * BLOCK, i * BLOCK + span)
        keep = keep_ref[i:i + 1, :] > 0.5
        grad_q, grad_k, grad_v = chunk_grads(
            q_ref[rows, :], do_ref[rows, :], kwin[keys, :], vwin[keys, :], keep, scale
        )
        dq_ref[rows, :] = grad_q.astype(dq_ref.dtype)
        dkwin[keys, :] += grad_k
        dvwin[keys, :] += grad_v
    dprev_ref[0] = dkwin[0:tokens, :].astype(dprev_ref.dtype)
    dprev_ref[1] = dvwin[0:tokens, :].astype(dprev_ref.dtype)
    down_ref[0] = dkwin[tokens:2 * tokens, :]
    down_ref[1] = dvwin[tokens:2 * tokens, :]
    dnext_ref[0] = dkwin[2 * tokens:3 * tokens, :].astype(dnext_ref.dtype)
    dnext_ref[1] = dvwin[2 * tokens:3 * tokens, :].astype(dnext_ref.dtype)


def col_kernel(q_ref, k_ref, v_ref, do_ref, keep_ref, out_ref):
    scale = HEAD_DIM ** (-0.5)
    keep = keep_ref[...] > 0.5
    grad_q, grad_k, grad_v = chunk_grads(
        q_ref[0], do_ref[0], k_ref[0], v_ref[0], keep, scale
    )
    out_ref[0] = grad_q.astype(out_ref.dtype)
    out_ref[1] = grad_k.astype(out_ref.dtype)
    out_ref[2] = grad_v.astype(out_ref.dtype)


def row_side(query_now, key_now, value_now, grad_now, near_before, near_after, keep):
    tokens = query_now.shape[0]
    span = (2 * REACH + 1) * BLOCK
    head_block = lambda h: (0, h)
    stacked_block = lambda part: pl.BlockSpec((None, tokens, HEAD_DIM), lambda h: (part, 0, h))
    plain = pl.BlockSpec((tokens, HEAD_DIM), head_block)
    pair_out = pl.BlockSpec((2, tokens, HEAD_DIM), lambda h: (0, 0, h))
    return pl.pallas_call(
        row_kernel,
        grid=(HEADS_ROW,),
        in_specs=[
            plain, plain,
            stacked_block(0), plain, stacked_block(0),
            stacked_block(1), plain, stacked_block(1),
            pl.BlockSpec(keep.shape, lambda h: (0, 0)),
        ],
        out_specs=[plain, pair_out, pair_out, pair_out],
        out_shape=[
            jax.ShapeDtypeStruct((tokens, HEADS_ROW * HEAD_DIM), jnp.bfloat16),
            jax.ShapeDtypeStruct((2, tokens, HEADS_ROW * HEAD_DIM), jnp.bfloat16),
            jax.ShapeDtypeStruct((2, tokens, HEADS_ROW * HEAD_DIM), jnp.float32),
            jax.ShapeDtypeStruct((2, tokens, HEADS_ROW * HEAD_DIM), jnp.bfloat16),
        ],
        scratch_shapes=[
            pltpu.VMEM((3 * tokens, HEAD_DIM), jnp.bfloat16),
            pltpu.VMEM((3 * tokens, HEAD_DIM), jnp.bfloat16),
            pltpu.VMEM((3 * tokens, HEAD_DIM), jnp.float32),
            pltpu.VMEM((3 * tokens, HEAD_DIM), jnp.float32),
        ],
    )(
        query_now, grad_now,
        near_before, key_now, near_after,
        near_before, value_now, near_after,
        keep,
    )


def col_side(received, keep):
    tokens = received.shape[1]
    part_block = lambda part: pl.BlockSpec((1, tokens, HEAD_DIM), lambda h: (part, 0, h))
    return pl.pallas_call(
        col_kernel,
        grid=(HEADS_COL,),
        in_specs=[
            part_block(0), part_block(1), part_block(2), part_block(3),
            pl.BlockSpec(keep.shape, lambda h: (0, 0)),
        ],
        out_specs=pl.BlockSpec((3, tokens, HEAD_DIM), lambda h: (0, 0, h)),
        out_shape=jax.ShapeDtypeStruct((3, tokens, HEADS_COL * HEAD_DIM), jnp.bfloat16),
    )(received, received, received, received, keep)


def body(query_act, key_act, value_act, out_grad, local_lists, strided_lists):
    devices = lax.axis_size("seq")
    position = lax.axis_index("seq")
    query_now = query_act[0]
    key_now = key_act[0]
    value_now = value_act[0]
    grad_now = out_grad[0]
    tokens = query_now.shape[0]
    block_count = tokens // BLOCK
    total_blocks = block_count * devices
    row_width = HEADS_ROW * HEAD_DIM
    share = tokens // devices

    near = jnp.stack([key_now[:, :row_width], value_now[:, :row_width]])
    near_before = shifted(near, "seq", 1)
    near_after = shifted(near, "seq", -1)
    sent = jnp.stack([item[:, row_width:] for item in (query_now, key_now, value_now, grad_now)])

    sent, near_before, near_after = lax.optimization_barrier((sent, near_before, near_after))
    received = lax.all_to_all(
        sent.reshape(4, share, devices, COLS), "seq", split_axis=2, concat_axis=1, tiled=True
    ).reshape(4, tokens, COLS)

    own_blocks = position * block_count + jnp.arange(block_count, dtype=jnp.int32)
    offsets = jnp.arange(-REACH, REACH + 1, dtype=jnp.int32)
    wanted = (own_blocks[:, None] + offsets[None, :]) % total_blocks
    row_allowed = jnp.any(wanted[:, :, None] == local_lists[:, None, :], axis=2)
    row_keep = jnp.repeat(row_allowed.astype(jnp.float32), BLOCK, axis=1)

    dq_row, d_prev, d_own, d_next = row_side(
        query_now, key_now, value_now, grad_now, near_before, near_after, row_keep
    )

    received, dq_row, d_prev, d_own, d_next = lax.optimization_barrier(
        (received, dq_row, d_prev, d_own, d_next)
    )
    from_after = shifted(d_prev, "seq", -1)
    from_before = shifted(d_next, "seq", 1)

    grid_rows = tokens * devices // COLS
    arrival = jnp.arange(tokens, dtype=jnp.int32)
    col_block = ((arrival % GROUP_COLS) * grid_rows + arrival // GROUP_COLS) // BLOCK
    local_strided = strided_lists - position * block_count
    listed = sum(
        (col_block == number)[:, None] * local_strided[number][None, :]
        for number in range(block_count)
    )
    col_keep = jnp.any(listed[:, :, None] == col_block[None, None, :], axis=1).astype(jnp.float32)
    col_grads = col_side(received, col_keep)

    col_grads, from_after, from_before = lax.optimization_barrier((col_grads, from_after, from_before))
    d_total = (d_own + from_before.astype(jnp.float32) + from_after.astype(jnp.float32)).astype(
        jnp.bfloat16
    )
    row_grads = jnp.concatenate([dq_row[None], d_total], axis=0)
    row_handed = shifted(row_grads, "pipe", -1)
    returned = lax.all_to_all(
        col_grads.reshape(3, devices, share, 1, COLS), "seq", split_axis=1, concat_axis=3, tiled=True
    ).reshape(3, tokens, COLS)
    col_handed = shifted(returned, "pipe", -1)

    handed = jnp.concatenate([row_handed, col_handed], axis=2)
    return (handed[0][None], handed[1][None], handed[2][None])


def solution(mesh):
    in_specs = (
        P("pipe", "seq", None),
        P("pipe", "seq", None),
        P("pipe", "seq", None),
        P("pipe", "seq", None),
        P("seq", None),
        P("seq", None),
    )
    out_specs = (P("pipe", "seq", None), P("pipe", "seq", None), P("pipe", "seq", None))
    return jax.shard_map(body, mesh=mesh, in_specs=in_specs, out_specs=out_specs, check_vma=False)
```

```python
import jax
import jax.numpy as jnp
from jax import lax
from jax.experimental import pallas as pl
from jax.experimental.pallas import tpu as pltpu
from jax.sharding import PartitionSpec as P

HEADS_ROW = 8
HEADS_COL = 8
HEAD_DIM = 128
COLS = 1024
BLOCK = 128
REACH = 3
GROUP_COLS = 16


def shifted(value, axis, steps):
    count = lax.axis_size(axis)
    pairs = [(source, (source + steps) % count) for source in range(count)]
    return lax.ppermute(value, axis, pairs)


def chunk_grads(q, do, k, v, keep, scale):
    scores = lax.dot_general(q, k, (((1,), (1,)), ((), ())), preferred_element_type=jnp.float32)
    scores = jnp.where(keep, scores * scale, -jnp.inf)
    largest = jnp.max(scores, axis=1, keepdims=True)
    raised = jnp.exp(scores - largest)
    softmax = raised / jnp.sum(raised, axis=1, keepdims=True)
    softmax_low = softmax.astype(jnp.bfloat16)
    attended = jnp.dot(softmax_low, v, preferred_element_type=jnp.float32)
    row_delta = jnp.sum(do.astype(jnp.float32) * attended, axis=1, keepdims=True)
    grad_softmax = lax.dot_general(
        do, v, (((1,), (1,)), ((), ())), preferred_element_type=jnp.float32
    )
    grad_scores = (scale * softmax * (grad_softmax - row_delta)).astype(jnp.bfloat16)
    grad_q = jnp.dot(grad_scores, k, preferred_element_type=jnp.float32)
    grad_k = lax.dot_general(
        grad_scores, q, (((0,), (0,)), ((), ())), preferred_element_type=jnp.float32
    )
    grad_v = lax.dot_general(
        softmax_low, do, (((0,), (0,)), ((), ())), preferred_element_type=jnp.float32
    )
    return grad_q, grad_k, grad_v


def row_kernel(
    q_ref, do_ref, kp_ref, ko_ref, kn_ref, vp_ref, vo_ref, vn_ref, keep_ref,
    dq_ref, dprev_ref, down_ref, dnext_ref, kwin, vwin, dkwin, dvwin,
):
    tokens = q_ref.shape[0]
    span = (2 * REACH + 1) * BLOCK
    scale = HEAD_DIM ** (-0.5)
    kwin[0:tokens, :] = kp_ref[...]
    kwin[tokens:2 * tokens, :] = ko_ref[...]
    kwin[2 * tokens:3 * tokens, :] = kn_ref[...]
    vwin[0:tokens, :] = vp_ref[...]
    vwin[tokens:2 * tokens, :] = vo_ref[...]
    vwin[2 * tokens:3 * tokens, :] = vn_ref[...]
    dkwin[...] = jnp.zeros_like(dkwin)
    dvwin[...] = jnp.zeros_like(dvwin)
    for i in range(tokens // BLOCK):
        rows = slice(i * BLOCK, (i + 1) * BLOCK)
        keys = slice(i * BLOCK, i * BLOCK + span)
        keep = keep_ref[i:i + 1, :] > 0.5
        grad_q, grad_k, grad_v = chunk_grads(
            q_ref[rows, :], do_ref[rows, :], kwin[keys, :], vwin[keys, :], keep, scale
        )
        dq_ref[rows, :] = grad_q.astype(dq_ref.dtype)
        dkwin[keys, :] += grad_k
        dvwin[keys, :] += grad_v
    dprev_ref[0] = dkwin[0:tokens, :].astype(dprev_ref.dtype)
    dprev_ref[1] = dvwin[0:tokens, :].astype(dprev_ref.dtype)
    down_ref[0] = dkwin[tokens:2 * tokens, :]
    down_ref[1] = dvwin[tokens:2 * tokens, :]
    dnext_ref[0] = dkwin[2 * tokens:3 * tokens, :].astype(dnext_ref.dtype)
    dnext_ref[1] = dvwin[2 * tokens:3 * tokens, :].astype(dnext_ref.dtype)


def col_kernel(q_ref, k_ref, v_ref, do_ref, keep_ref, out_ref):
    scale = HEAD_DIM ** (-0.5)
    keep = keep_ref[...] > 0.5
    grad_q, grad_k, grad_v = chunk_grads(
        q_ref[0], do_ref[0], k_ref[0], v_ref[0], keep, scale
    )
    out_ref[0] = grad_q.astype(out_ref.dtype)
    out_ref[1] = grad_k.astype(out_ref.dtype)
    out_ref[2] = grad_v.astype(out_ref.dtype)


def row_side(query_now, key_now, value_now, grad_now, near_before, near_after, keep):
    tokens = query_now.shape[0]
    span = (2 * REACH + 1) * BLOCK
    head_block = lambda h: (0, h)
    stacked_block = lambda part: pl.BlockSpec((None, tokens, HEAD_DIM), lambda h: (part, 0, h))
    plain = pl.BlockSpec((tokens, HEAD_DIM), head_block)
    pair_out = pl.BlockSpec((2, tokens, HEAD_DIM), lambda h: (0, 0, h))
    return pl.pallas_call(
        row_kernel,
        grid=(HEADS_ROW,),
        in_specs=[
            plain, plain,
            stacked_block(0), plain, stacked_block(0),
            stacked_block(1), plain, stacked_block(1),
            pl.BlockSpec(keep.shape, lambda h: (0, 0)),
        ],
        out_specs=[plain, pair_out, pair_out, pair_out],
        out_shape=[
            jax.ShapeDtypeStruct((tokens, HEADS_ROW * HEAD_DIM), jnp.bfloat16),
            jax.ShapeDtypeStruct((2, tokens, HEADS_ROW * HEAD_DIM), jnp.bfloat16),
            jax.ShapeDtypeStruct((2, tokens, HEADS_ROW * HEAD_DIM), jnp.float32),
            jax.ShapeDtypeStruct((2, tokens, HEADS_ROW * HEAD_DIM), jnp.bfloat16),
        ],
        scratch_shapes=[
            pltpu.VMEM((3 * tokens, HEAD_DIM), jnp.bfloat16),
            pltpu.VMEM((3 * tokens, HEAD_DIM), jnp.bfloat16),
            pltpu.VMEM((3 * tokens, HEAD_DIM), jnp.float32),
            pltpu.VMEM((3 * tokens, HEAD_DIM), jnp.float32),
        ],
    )(
        query_now, grad_now,
        near_before, key_now, near_after,
        near_before, value_now, near_after,
        keep,
    )


def col_side(received, keep):
    tokens = received.shape[1]
    part_block = lambda part: pl.BlockSpec((1, tokens, HEAD_DIM), lambda h: (part, 0, h))
    return pl.pallas_call(
        col_kernel,
        grid=(HEADS_COL,),
        in_specs=[
            part_block(0), part_block(1), part_block(2), part_block(3),
            pl.BlockSpec(keep.shape, lambda h: (0, 0)),
        ],
        out_specs=pl.BlockSpec((3, tokens, HEAD_DIM), lambda h: (0, 0, h)),
        out_shape=jax.ShapeDtypeStruct((3, tokens, HEADS_COL * HEAD_DIM), jnp.bfloat16),
    )(received, received, received, received, keep)


def body(query_act, key_act, value_act, out_grad, local_lists, strided_lists):
    devices = lax.axis_size("seq")
    position = lax.axis_index("seq")
    query_now = query_act[0]
    key_now = key_act[0]
    value_now = value_act[0]
    grad_now = out_grad[0]
    tokens = query_now.shape[0]
    block_count = tokens // BLOCK
    total_blocks = block_count * devices
    row_width = HEADS_ROW * HEAD_DIM
    share = tokens // devices

    near = jnp.stack([key_now[:, :row_width], value_now[:, :row_width]])
    near_before = shifted(near, "seq", 1)
    near_after = shifted(near, "seq", -1)
    sent = jnp.stack([item[:, row_width:] for item in (query_now, key_now, value_now, grad_now)])

    sent, near_before, near_after = lax.optimization_barrier((sent, near_before, near_after))
    received = lax.all_to_all(
        sent.reshape(4, share, devices, COLS), "seq", split_axis=2, concat_axis=1, tiled=True
    ).reshape(4, tokens, COLS)

    own_blocks = position * block_count + jnp.arange(block_count, dtype=jnp.int32)
    offsets = jnp.arange(-REACH, REACH + 1, dtype=jnp.int32)
    wanted = (own_blocks[:, None] + offsets[None, :]) % total_blocks
    row_allowed = jnp.any(wanted[:, :, None] == local_lists[:, None, :], axis=2)
    row_keep = jnp.repeat(row_allowed.astype(jnp.float32), BLOCK, axis=1)

    dq_row, d_prev, d_own, d_next = row_side(
        query_now, key_now, value_now, grad_now, near_before, near_after, row_keep
    )

    received, dq_row, d_prev, d_own, d_next = lax.optimization_barrier(
        (received, dq_row, d_prev, d_own, d_next)
    )
    from_after = shifted(d_prev, "seq", -1)
    from_before = shifted(d_next, "seq", 1)

    grid_rows = tokens * devices // COLS
    arrival = jnp.arange(tokens, dtype=jnp.int32)
    col_block = ((arrival % GROUP_COLS) * grid_rows + arrival // GROUP_COLS) // BLOCK
    local_strided = strided_lists - position * block_count
    listed = sum(
        (col_block == number)[:, None] * local_strided[number][None, :]
        for number in range(block_count)
    )
    col_keep = jnp.any(listed[:, :, None] == col_block[None, None, :], axis=1).astype(jnp.float32)
    col_grads = shifted(col_side(received, col_keep), "pipe", -1)

    col_grads, from_after, from_before = lax.optimization_barrier((col_grads, from_after, from_before))
    d_total = (d_own + from_before.astype(jnp.float32) + from_after.astype(jnp.float32)).astype(
        jnp.bfloat16
    )
    row_grads = jnp.concatenate([dq_row[None], d_total], axis=0)
    row_handed = shifted(row_grads, "pipe", -1)
    col_handed = lax.all_to_all(
        col_grads.reshape(3, devices, share, 1, COLS), "seq", split_axis=1, concat_axis=3, tiled=True
    ).reshape(3, tokens, COLS)

    handed = jnp.concatenate([row_handed, col_handed], axis=2)
    return (handed[0][None], handed[1][None], handed[2][None])


def solution(mesh):
    in_specs = (
        P("pipe", "seq", None),
        P("pipe", "seq", None),
        P("pipe", "seq", None),
        P("pipe", "seq", None),
        P("seq", None),
        P("seq", None),
    )
    out_specs = (P("pipe", "seq", None), P("pipe", "seq", None), P("pipe", "seq", None))
    return jax.shard_map(body, mesh=mesh, in_specs=in_specs, out_specs=out_specs, check_vma=False)
```

```python
import jax
import jax.numpy as jnp
from jax import lax
from jax.experimental import pallas as pl
from jax.experimental.pallas import tpu as pltpu
from jax.sharding import PartitionSpec as P

HEADS_ROW = 8
HEADS_COL = 8
HEAD_DIM = 128
COLS = 1024
BLOCK = 128
REACH = 3
GROUP_COLS = 16


def shifted(value, axis, steps):
    count = lax.axis_size(axis)
    pairs = [(source, (source + steps) % count) for source in range(count)]
    return lax.ppermute(value, axis, pairs)


def chunk_grads(q, do, k, v, keep, scale):
    scores = lax.dot_general(q, k, (((1,), (1,)), ((), ())), preferred_element_type=jnp.float32)
    scores = jnp.where(keep, scores * scale, -jnp.inf)
    largest = jnp.max(scores, axis=1, keepdims=True)
    raised = jnp.exp(scores - largest)
    softmax = raised / jnp.sum(raised, axis=1, keepdims=True)
    softmax_low = softmax.astype(jnp.bfloat16)
    attended = jnp.dot(softmax_low, v, preferred_element_type=jnp.float32)
    row_delta = jnp.sum(do.astype(jnp.float32) * attended, axis=1, keepdims=True)
    grad_softmax = lax.dot_general(
        do, v, (((1,), (1,)), ((), ())), preferred_element_type=jnp.float32
    )
    grad_scores = (scale * softmax * (grad_softmax - row_delta)).astype(jnp.bfloat16)
    grad_q = jnp.dot(grad_scores, k, preferred_element_type=jnp.float32)
    grad_k = lax.dot_general(
        grad_scores, q, (((0,), (0,)), ((), ())), preferred_element_type=jnp.float32
    )
    grad_v = lax.dot_general(
        softmax_low, do, (((0,), (0,)), ((), ())), preferred_element_type=jnp.float32
    )
    return grad_q, grad_k, grad_v


def row_kernel(
    q_ref, do_ref, kp_ref, ko_ref, kn_ref, vp_ref, vo_ref, vn_ref, keep_ref,
    dq_ref, dprev_ref, down_ref, dnext_ref, kwin, vwin, dkwin, dvwin,
):
    tokens = q_ref.shape[0]
    span = (2 * REACH + 1) * BLOCK
    scale = HEAD_DIM ** (-0.5)
    kwin[0:tokens, :] = kp_ref[...]
    kwin[tokens:2 * tokens, :] = ko_ref[...]
    kwin[2 * tokens:3 * tokens, :] = kn_ref[...]
    vwin[0:tokens, :] = vp_ref[...]
    vwin[tokens:2 * tokens, :] = vo_ref[...]
    vwin[2 * tokens:3 * tokens, :] = vn_ref[...]
    dkwin[...] = jnp.zeros_like(dkwin)
    dvwin[...] = jnp.zeros_like(dvwin)
    for i in range(tokens // BLOCK):
        rows = slice(i * BLOCK, (i + 1) * BLOCK)
        keys = slice(i * BLOCK, i * BLOCK + span)
        keep = keep_ref[i:i + 1, :] > 0.5
        grad_q, grad_k, grad_v = chunk_grads(
            q_ref[rows, :], do_ref[rows, :], kwin[keys, :], vwin[keys, :], keep, scale
        )
        dq_ref[rows, :] = grad_q.astype(dq_ref.dtype)
        dkwin[keys, :] += grad_k
        dvwin[keys, :] += grad_v
    dprev_ref[0] = dkwin[0:tokens, :].astype(dprev_ref.dtype)
    dprev_ref[1] = dvwin[0:tokens, :].astype(dprev_ref.dtype)
    down_ref[0] = dkwin[tokens:2 * tokens, :]
    down_ref[1] = dvwin[tokens:2 * tokens, :]
    dnext_ref[0] = dkwin[2 * tokens:3 * tokens, :].astype(dnext_ref.dtype)
    dnext_ref[1] = dvwin[2 * tokens:3 * tokens, :].astype(dnext_ref.dtype)


def col_kernel(q_ref, k_ref, v_ref, do_ref, keep_ref, out_ref):
    scale = HEAD_DIM ** (-0.5)
    keep = keep_ref[...] > 0.5
    grad_q, grad_k, grad_v = chunk_grads(
        q_ref[0], do_ref[0], k_ref[0], v_ref[0], keep, scale
    )
    out_ref[0] = grad_q.astype(out_ref.dtype)
    out_ref[1] = grad_k.astype(out_ref.dtype)
    out_ref[2] = grad_v.astype(out_ref.dtype)


def row_side(query_now, key_now, value_now, grad_now, near_before, near_after, keep):
    tokens = query_now.shape[0]
    span = (2 * REACH + 1) * BLOCK
    head_block = lambda h: (0, h)
    stacked_block = lambda part: pl.BlockSpec((None, tokens, HEAD_DIM), lambda h: (part, 0, h))
    plain = pl.BlockSpec((tokens, HEAD_DIM), head_block)
    pair_out = pl.BlockSpec((2, tokens, HEAD_DIM), lambda h: (0, 0, h))
    return pl.pallas_call(
        row_kernel,
        grid=(HEADS_ROW,),
        in_specs=[
            plain, plain,
            stacked_block(0), plain, stacked_block(0),
            stacked_block(1), plain, stacked_block(1),
            pl.BlockSpec(keep.shape, lambda h: (0, 0)),
        ],
        out_specs=[plain, pair_out, pair_out, pair_out],
        out_shape=[
            jax.ShapeDtypeStruct((tokens, HEADS_ROW * HEAD_DIM), jnp.bfloat16),
            jax.ShapeDtypeStruct((2, tokens, HEADS_ROW * HEAD_DIM), jnp.bfloat16),
            jax.ShapeDtypeStruct((2, tokens, HEADS_ROW * HEAD_DIM), jnp.float32),
            jax.ShapeDtypeStruct((2, tokens, HEADS_ROW * HEAD_DIM), jnp.bfloat16),
        ],
        scratch_shapes=[
            pltpu.VMEM((3 * tokens, HEAD_DIM), jnp.bfloat16),
            pltpu.VMEM((3 * tokens, HEAD_DIM), jnp.bfloat16),
            pltpu.VMEM((3 * tokens, HEAD_DIM), jnp.float32),
            pltpu.VMEM((3 * tokens, HEAD_DIM), jnp.float32),
        ],
    )(
        query_now, grad_now,
        near_before, key_now, near_after,
        near_before, value_now, near_after,
        keep,
    )


def col_side(received, keep):
    tokens = received.shape[1]
    part_block = lambda part: pl.BlockSpec((1, tokens, HEAD_DIM), lambda h: (part, 0, h))
    return pl.pallas_call(
        col_kernel,
        grid=(HEADS_COL,),
        in_specs=[
            part_block(0), part_block(1), part_block(2), part_block(3),
            pl.BlockSpec(keep.shape, lambda h: (0, 0)),
        ],
        out_specs=pl.BlockSpec((3, tokens, HEAD_DIM), lambda h: (0, 0, h)),
        out_shape=jax.ShapeDtypeStruct((3, tokens, HEADS_COL * HEAD_DIM), jnp.bfloat16),
    )(received, received, received, received, keep)


def body(query_act, key_act, value_act, out_grad, local_lists, strided_lists):
    devices = lax.axis_size("seq")
    position = lax.axis_index("seq")
    query_now = query_act[0]
    key_now = key_act[0]
    value_now = value_act[0]
    grad_now = out_grad[0]
    tokens = query_now.shape[0]
    block_count = tokens // BLOCK
    total_blocks = block_count * devices
    row_width = HEADS_ROW * HEAD_DIM
    share = tokens // devices

    near = jnp.stack([key_now[:, :row_width], value_now[:, :row_width]])
    near_before = shifted(near, "seq", 1)
    near_after = shifted(near, "seq", -1)
    sent = jnp.stack([item[:, row_width:] for item in (query_now, key_now, value_now, grad_now)])

    sent = sent.reshape(4, share, devices, COLS)
    sent, near_before, near_after = lax.optimization_barrier((sent, near_before, near_after))
    received = lax.all_to_all(
        sent, "seq", split_axis=2, concat_axis=1, tiled=True
    ).reshape(4, tokens, COLS)

    own_blocks = position * block_count + jnp.arange(block_count, dtype=jnp.int32)
    offsets = jnp.arange(-REACH, REACH + 1, dtype=jnp.int32)
    wanted = (own_blocks[:, None] + offsets[None, :]) % total_blocks
    row_allowed = jnp.any(wanted[:, :, None] == local_lists[:, None, :], axis=2)
    row_keep = jnp.repeat(row_allowed.astype(jnp.float32), BLOCK, axis=1)

    dq_row, d_prev, d_own, d_next = row_side(
        query_now, key_now, value_now, grad_now, near_before, near_after, row_keep
    )

    received, dq_row, d_prev, d_own, d_next = lax.optimization_barrier(
        (received, dq_row, d_prev, d_own, d_next)
    )
    from_after = shifted(d_prev, "seq", -1)
    from_before = shifted(d_next, "seq", 1)

    grid_rows = tokens * devices // COLS
    arrival = jnp.arange(tokens, dtype=jnp.int32)
    col_block = ((arrival % GROUP_COLS) * grid_rows + arrival // GROUP_COLS) // BLOCK
    local_strided = strided_lists - position * block_count
    listed = sum(
        (col_block == number)[:, None] * local_strided[number][None, :]
        for number in range(block_count)
    )
    col_keep = jnp.any(listed[:, :, None] == col_block[None, None, :], axis=1).astype(jnp.float32)
    col_grads = col_side(received, col_keep).reshape(3, devices, share, 1, COLS)

    col_grads, from_after, from_before = lax.optimization_barrier((col_grads, from_after, from_before))
    d_total = (d_own + from_before.astype(jnp.float32) + from_after.astype(jnp.float32)).astype(
        jnp.bfloat16
    )
    row_grads = jnp.concatenate([dq_row[None], d_total], axis=0)
    row_handed = shifted(row_grads, "pipe", -1)
    returned = lax.all_to_all(
        col_grads, "seq", split_axis=1, concat_axis=3, tiled=True
    ).reshape(3, tokens, COLS)
    col_handed = shifted(returned, "pipe", -1)

    handed = jnp.concatenate([row_handed, col_handed], axis=2)
    return (handed[0][None], handed[1][None], handed[2][None])


def solution(mesh):
    in_specs = (
        P("pipe", "seq", None),
        P("pipe", "seq", None),
        P("pipe", "seq", None),
        P("pipe", "seq", None),
        P("seq", None),
        P("seq", None),
    )
    out_specs = (P("pipe", "seq", None), P("pipe", "seq", None), P("pipe", "seq", None))
    return jax.shard_map(body, mesh=mesh, in_specs=in_specs, out_specs=out_specs, check_vma=False)
```

```python
import jax
import jax.numpy as jnp
from jax import lax
from jax.experimental import pallas as pl
from jax.experimental.pallas import tpu as pltpu
from jax.sharding import PartitionSpec as P

HEADS_ROW = 8
HEADS_COL = 8
HEAD_DIM = 128
COLS = 1024
BLOCK = 128
REACH = 3
GROUP_COLS = 16


def shifted(value, axis, steps):
    count = lax.axis_size(axis)
    pairs = [(source, (source + steps) % count) for source in range(count)]
    return lax.ppermute(value, axis, pairs)


def chunk_grads(q, do, k, v, keep, scale):
    scores = lax.dot_general(q, k, (((1,), (1,)), ((), ())), preferred_element_type=jnp.float32)
    scores = jnp.where(keep, scores * scale, -jnp.inf)
    largest = jnp.max(scores, axis=1, keepdims=True)
    raised = jnp.exp(scores - largest)
    softmax = raised / jnp.sum(raised, axis=1, keepdims=True)
    softmax_low = softmax.astype(jnp.bfloat16)
    attended = jnp.dot(softmax_low, v, preferred_element_type=jnp.float32)
    row_delta = jnp.sum(do.astype(jnp.float32) * attended, axis=1, keepdims=True)
    grad_softmax = lax.dot_general(
        do, v, (((1,), (1,)), ((), ())), preferred_element_type=jnp.float32
    )
    grad_scores = (scale * softmax * (grad_softmax - row_delta)).astype(jnp.bfloat16)
    grad_q = jnp.dot(grad_scores, k, preferred_element_type=jnp.float32)
    grad_k = lax.dot_general(
        grad_scores, q, (((0,), (0,)), ((), ())), preferred_element_type=jnp.float32
    )
    grad_v = lax.dot_general(
        softmax_low, do, (((0,), (0,)), ((), ())), preferred_element_type=jnp.float32
    )
    return grad_q, grad_k, grad_v


def row_kernel(
    q_ref, do_ref, kp_ref, ko_ref, kn_ref, vp_ref, vo_ref, vn_ref, keep_ref,
    dq_ref, dprev_ref, down_ref, dnext_ref, kwin, vwin, dkwin, dvwin,
):
    tokens = q_ref.shape[0]
    span = (2 * REACH + 1) * BLOCK
    scale = HEAD_DIM ** (-0.5)
    kwin[0:tokens, :] = kp_ref[...]
    kwin[tokens:2 * tokens, :] = ko_ref[...]
    kwin[2 * tokens:3 * tokens, :] = kn_ref[...]
    vwin[0:tokens, :] = vp_ref[...]
    vwin[tokens:2 * tokens, :] = vo_ref[...]
    vwin[2 * tokens:3 * tokens, :] = vn_ref[...]
    dkwin[...] = jnp.zeros_like(dkwin)
    dvwin[...] = jnp.zeros_like(dvwin)
    for i in range(tokens // BLOCK):
        rows = slice(i * BLOCK, (i + 1) * BLOCK)
        keys = slice(i * BLOCK, i * BLOCK + span)
        keep = keep_ref[i:i + 1, :] > 0.5
        grad_q, grad_k, grad_v = chunk_grads(
            q_ref[rows, :], do_ref[rows, :], kwin[keys, :], vwin[keys, :], keep, scale
        )
        dq_ref[rows, :] = grad_q.astype(dq_ref.dtype)
        dkwin[keys, :] += grad_k
        dvwin[keys, :] += grad_v
    dprev_ref[0] = dkwin[0:tokens, :].astype(dprev_ref.dtype)
    dprev_ref[1] = dvwin[0:tokens, :].astype(dprev_ref.dtype)
    down_ref[0] = dkwin[tokens:2 * tokens, :]
    down_ref[1] = dvwin[tokens:2 * tokens, :]
    dnext_ref[0] = dkwin[2 * tokens:3 * tokens, :].astype(dnext_ref.dtype)
    dnext_ref[1] = dvwin[2 * tokens:3 * tokens, :].astype(dnext_ref.dtype)


def col_kernel(q_ref, k_ref, v_ref, do_ref, keep_ref, out_ref):
    scale = HEAD_DIM ** (-0.5)
    keep = keep_ref[...] > 0.5
    grad_q, grad_k, grad_v = chunk_grads(
        q_ref[0], do_ref[0], k_ref[0], v_ref[0], keep, scale
    )
    out_ref[0] = grad_q.astype(out_ref.dtype)
    out_ref[1] = grad_k.astype(out_ref.dtype)
    out_ref[2] = grad_v.astype(out_ref.dtype)


def row_side(query_now, key_now, value_now, grad_now, near_before, near_after, keep):
    tokens = query_now.shape[0]
    span = (2 * REACH + 1) * BLOCK
    head_block = lambda h: (0, h)
    stacked_block = lambda part: pl.BlockSpec((None, tokens, HEAD_DIM), lambda h: (part, 0, h))
    plain = pl.BlockSpec((tokens, HEAD_DIM), head_block)
    pair_out = pl.BlockSpec((2, tokens, HEAD_DIM), lambda h: (0, 0, h))
    return pl.pallas_call(
        row_kernel,
        grid=(HEADS_ROW,),
        in_specs=[
            plain, plain,
            stacked_block(0), plain, stacked_block(0),
            stacked_block(1), plain, stacked_block(1),
            pl.BlockSpec(keep.shape, lambda h: (0, 0)),
        ],
        out_specs=[plain, pair_out, pair_out, pair_out],
        out_shape=[
            jax.ShapeDtypeStruct((tokens, HEADS_ROW * HEAD_DIM), jnp.bfloat16),
            jax.ShapeDtypeStruct((2, tokens, HEADS_ROW * HEAD_DIM), jnp.bfloat16),
            jax.ShapeDtypeStruct((2, tokens, HEADS_ROW * HEAD_DIM), jnp.float32),
            jax.ShapeDtypeStruct((2, tokens, HEADS_ROW * HEAD_DIM), jnp.bfloat16),
        ],
        scratch_shapes=[
            pltpu.VMEM((3 * tokens, HEAD_DIM), jnp.bfloat16),
            pltpu.VMEM((3 * tokens, HEAD_DIM), jnp.bfloat16),
            pltpu.VMEM((3 * tokens, HEAD_DIM), jnp.float32),
            pltpu.VMEM((3 * tokens, HEAD_DIM), jnp.float32),
        ],
    )(
        query_now, grad_now,
        near_before, key_now, near_after,
        near_before, value_now, near_after,
        keep,
    )


def col_side(received, keep):
    tokens = received.shape[1]
    part_block = lambda part: pl.BlockSpec((1, tokens, HEAD_DIM), lambda h: (part, 0, h))
    return pl.pallas_call(
        col_kernel,
        grid=(HEADS_COL,),
        in_specs=[
            part_block(0), part_block(1), part_block(2), part_block(3),
            pl.BlockSpec(keep.shape, lambda h: (0, 0)),
        ],
        out_specs=pl.BlockSpec((3, tokens, HEAD_DIM), lambda h: (0, 0, h)),
        out_shape=jax.ShapeDtypeStruct((3, tokens, HEADS_COL * HEAD_DIM), jnp.bfloat16),
    )(received, received, received, received, keep)


def body(query_act, key_act, value_act, out_grad, local_lists, strided_lists):
    devices = lax.axis_size("seq")
    position = lax.axis_index("seq")
    query_now = query_act[0]
    key_now = key_act[0]
    value_now = value_act[0]
    grad_now = out_grad[0]
    tokens = query_now.shape[0]
    block_count = tokens // BLOCK
    total_blocks = block_count * devices
    row_width = HEADS_ROW * HEAD_DIM
    share = tokens // devices

    near = jnp.stack([key_now[:, :row_width], value_now[:, :row_width]])
    near_before = shifted(near, "seq", 1)
    near_after = shifted(near, "seq", -1)
    sent = jnp.stack([item[:, row_width:] for item in (query_now, key_now, value_now, grad_now)])

    sent = sent.reshape(4, share, devices, COLS)
    sent, near_before, near_after = lax.optimization_barrier((sent, near_before, near_after))
    received = lax.all_to_all(
        sent, "seq", split_axis=2, concat_axis=1, tiled=True
    ).reshape(4, tokens, COLS)

    own_blocks = position * block_count + jnp.arange(block_count, dtype=jnp.int32)
    offsets = jnp.arange(-REACH, REACH + 1, dtype=jnp.int32)
    wanted = (own_blocks[:, None] + offsets[None, :]) % total_blocks
    row_allowed = jnp.any(wanted[:, :, None] == local_lists[:, None, :], axis=2)
    row_keep = jnp.repeat(row_allowed.astype(jnp.float32), BLOCK, axis=1)

    dq_row, d_prev, d_own, d_next = row_side(
        query_now, key_now, value_now, grad_now, near_before, near_after, row_keep
    )

    received, dq_row, d_prev, d_own, d_next = lax.optimization_barrier(
        (received, dq_row, d_prev, d_own, d_next)
    )
    from_after = shifted(d_prev, "seq", -1)
    from_before = shifted(d_next, "seq", 1)

    grid_rows = tokens * devices // COLS
    arrival = jnp.arange(tokens, dtype=jnp.int32)
    col_block = ((arrival % GROUP_COLS) * grid_rows + arrival // GROUP_COLS) // BLOCK
    local_strided = strided_lists - position * block_count
    listed = sum(
        (col_block == number)[:, None] * local_strided[number][None, :]
        for number in range(block_count)
    )
    col_keep = jnp.any(listed[:, :, None] == col_block[None, None, :], axis=1).astype(jnp.float32)
    col_grads = col_side(received, col_keep).reshape(3, devices, share, 1, COLS)

    col_grads, from_after, from_before = lax.optimization_barrier((col_grads, from_after, from_before))
    d_total = (d_own + from_before.astype(jnp.float32) + from_after.astype(jnp.float32)).astype(
        jnp.bfloat16
    )
    row_grads = jnp.concatenate([dq_row[None], d_total], axis=0)
    row_handed = shifted(row_grads, "pipe", -1)
    returned = lax.all_to_all(col_grads, "seq", split_axis=1, concat_axis=3, tiled=True)
    col_handed = shifted(returned, "pipe", -1).reshape(3, tokens, COLS)

    handed = jnp.concatenate([row_handed, col_handed], axis=2)
    return (handed[0][None], handed[1][None], handed[2][None])


def solution(mesh):
    in_specs = (
        P("pipe", "seq", None),
        P("pipe", "seq", None),
        P("pipe", "seq", None),
        P("pipe", "seq", None),
        P("seq", None),
        P("seq", None),
    )
    out_specs = (P("pipe", "seq", None), P("pipe", "seq", None), P("pipe", "seq", None))
    return jax.shard_map(body, mesh=mesh, in_specs=in_specs, out_specs=out_specs, check_vma=False)
```

```python
import jax
import jax.numpy as jnp
from jax import lax
from jax.experimental import pallas as pl
from jax.experimental.pallas import tpu as pltpu
from jax.sharding import PartitionSpec as P

HEADS_ROW = 8
HEADS_COL = 8
HEAD_DIM = 128
COLS = 1024
BLOCK = 128
REACH = 3
GROUP_COLS = 16


def shifted(value, axis, steps):
    count = lax.axis_size(axis)
    pairs = [(source, (source + steps) % count) for source in range(count)]
    return lax.ppermute(value, axis, pairs)


def chunk_grads(q, do, k, v, keep, scale):
    scores = lax.dot_general(q, k, (((1,), (1,)), ((), ())), preferred_element_type=jnp.float32)
    scores = jnp.where(keep, scores * scale, -jnp.inf)
    largest = jnp.max(scores, axis=1, keepdims=True)
    raised = jnp.exp(scores - largest)
    softmax = raised / jnp.sum(raised, axis=1, keepdims=True)
    softmax_low = softmax.astype(jnp.bfloat16)
    attended = jnp.dot(softmax_low, v, preferred_element_type=jnp.float32)
    row_delta = jnp.sum(do.astype(jnp.float32) * attended, axis=1, keepdims=True)
    grad_softmax = lax.dot_general(
        do, v, (((1,), (1,)), ((), ())), preferred_element_type=jnp.float32
    )
    grad_scores = (scale * softmax * (grad_softmax - row_delta)).astype(jnp.bfloat16)
    grad_q = jnp.dot(grad_scores, k, preferred_element_type=jnp.float32)
    grad_k = lax.dot_general(
        grad_scores, q, (((0,), (0,)), ((), ())), preferred_element_type=jnp.float32
    )
    grad_v = lax.dot_general(
        softmax_low, do, (((0,), (0,)), ((), ())), preferred_element_type=jnp.float32
    )
    return grad_q, grad_k, grad_v


def row_kernel(
    q_ref, do_ref, kp_ref, ko_ref, kn_ref, vp_ref, vo_ref, vn_ref, keep_ref,
    dq_ref, dprev_ref, down_ref, dnext_ref, kwin, vwin, dkwin, dvwin,
):
    tokens = q_ref.shape[0]
    span = (2 * REACH + 1) * BLOCK
    scale = HEAD_DIM ** (-0.5)
    kwin[0:tokens, :] = kp_ref[...]
    kwin[tokens:2 * tokens, :] = ko_ref[...]
    kwin[2 * tokens:3 * tokens, :] = kn_ref[...]
    vwin[0:tokens, :] = vp_ref[...]
    vwin[tokens:2 * tokens, :] = vo_ref[...]
    vwin[2 * tokens:3 * tokens, :] = vn_ref[...]
    dkwin[...] = jnp.zeros_like(dkwin)
    dvwin[...] = jnp.zeros_like(dvwin)
    for i in range(tokens // BLOCK):
        rows = slice(i * BLOCK, (i + 1) * BLOCK)
        keys = slice(i * BLOCK, i * BLOCK + span)
        keep = keep_ref[i:i + 1, :] > 0.5
        grad_q, grad_k, grad_v = chunk_grads(
            q_ref[rows, :], do_ref[rows, :], kwin[keys, :], vwin[keys, :], keep, scale
        )
        dq_ref[rows, :] = grad_q.astype(dq_ref.dtype)
        dkwin[keys, :] += grad_k
        dvwin[keys, :] += grad_v
    dprev_ref[0] = dkwin[0:tokens, :].astype(dprev_ref.dtype)
    dprev_ref[1] = dvwin[0:tokens, :].astype(dprev_ref.dtype)
    down_ref[0] = dkwin[tokens:2 * tokens, :]
    down_ref[1] = dvwin[tokens:2 * tokens, :]
    dnext_ref[0] = dkwin[2 * tokens:3 * tokens, :].astype(dnext_ref.dtype)
    dnext_ref[1] = dvwin[2 * tokens:3 * tokens, :].astype(dnext_ref.dtype)


def col_kernel(q_ref, k_ref, v_ref, do_ref, keep_ref, out_ref):
    scale = HEAD_DIM ** (-0.5)
    keep = keep_ref[...] > 0.5
    grad_q, grad_k, grad_v = chunk_grads(
        q_ref[0], do_ref[0], k_ref[0], v_ref[0], keep, scale
    )
    out_ref[0] = grad_q.astype(out_ref.dtype)
    out_ref[1] = grad_k.astype(out_ref.dtype)
    out_ref[2] = grad_v.astype(out_ref.dtype)


def row_side(query_now, key_now, value_now, grad_now, near_before, near_after, keep):
    tokens = query_now.shape[0]
    span = (2 * REACH + 1) * BLOCK
    head_block = lambda h: (0, h)
    stacked_block = lambda part: pl.BlockSpec((None, tokens, HEAD_DIM), lambda h: (part, 0, h))
    plain = pl.BlockSpec((tokens, HEAD_DIM), head_block)
    pair_out = pl.BlockSpec((2, tokens, HEAD_DIM), lambda h: (0, 0, h))
    return pl.pallas_call(
        row_kernel,
        grid=(HEADS_ROW,),
        in_specs=[
            plain, plain,
            stacked_block(0), plain, stacked_block(0),
            stacked_block(1), plain, stacked_block(1),
            pl.BlockSpec(keep.shape, lambda h: (0, 0)),
        ],
        out_specs=[plain, pair_out, pair_out, pair_out],
        out_shape=[
            jax.ShapeDtypeStruct((tokens, HEADS_ROW * HEAD_DIM), jnp.bfloat16),
            jax.ShapeDtypeStruct((2, tokens, HEADS_ROW * HEAD_DIM), jnp.bfloat16),
            jax.ShapeDtypeStruct((2, tokens, HEADS_ROW * HEAD_DIM), jnp.float32),
            jax.ShapeDtypeStruct((2, tokens, HEADS_ROW * HEAD_DIM), jnp.bfloat16),
        ],
        scratch_shapes=[
            pltpu.VMEM((3 * tokens, HEAD_DIM), jnp.bfloat16),
            pltpu.VMEM((3 * tokens, HEAD_DIM), jnp.bfloat16),
            pltpu.VMEM((3 * tokens, HEAD_DIM), jnp.float32),
            pltpu.VMEM((3 * tokens, HEAD_DIM), jnp.float32),
        ],
    )(
        query_now, grad_now,
        near_before, key_now, near_after,
        near_before, value_now, near_after,
        keep,
    )


def col_side(received, keep):
    tokens = received.shape[1]
    part_block = lambda part: pl.BlockSpec((1, tokens, HEAD_DIM), lambda h: (part, 0, h))
    return pl.pallas_call(
        col_kernel,
        grid=(HEADS_COL,),
        in_specs=[
            part_block(0), part_block(1), part_block(2), part_block(3),
            pl.BlockSpec(keep.shape, lambda h: (0, 0)),
        ],
        out_specs=pl.BlockSpec((3, tokens, HEAD_DIM), lambda h: (0, 0, h)),
        out_shape=jax.ShapeDtypeStruct((3, tokens, HEADS_COL * HEAD_DIM), jnp.bfloat16),
    )(received, received, received, received, keep)


def body(query_act, key_act, value_act, out_grad, local_lists, strided_lists):
    devices = lax.axis_size("seq")
    position = lax.axis_index("seq")
    query_now = query_act[0]
    key_now = key_act[0]
    value_now = value_act[0]
    grad_now = out_grad[0]
    tokens = query_now.shape[0]
    block_count = tokens // BLOCK
    total_blocks = block_count * devices
    row_width = HEADS_ROW * HEAD_DIM
    share = tokens // devices

    near = jnp.stack([key_now[:, :row_width], value_now[:, :row_width]])
    near_before = shifted(near, "seq", 1)
    near_after = shifted(near, "seq", -1)
    sent = jnp.stack([item[:, row_width:] for item in (query_now, key_now, value_now, grad_now)])

    sent = sent.reshape(4, share, devices, COLS)
    sent, near_before, near_after = lax.optimization_barrier((sent, near_before, near_after))
    received = lax.all_to_all(
        sent, "seq", split_axis=2, concat_axis=1, tiled=True
    ).reshape(4, tokens, COLS)

    own_blocks = position * block_count + jnp.arange(block_count, dtype=jnp.int32)
    offsets = jnp.arange(-REACH, REACH + 1, dtype=jnp.int32)
    wanted = (own_blocks[:, None] + offsets[None, :]) % total_blocks
    row_allowed = jnp.any(wanted[:, :, None] == local_lists[:, None, :], axis=2)
    row_keep = jnp.repeat(row_allowed.astype(jnp.float32), BLOCK, axis=1)

    dq_row, d_prev, d_own, d_next = row_side(
        query_now, key_now, value_now, grad_now, near_before, near_after, row_keep
    )

    received, dq_row, d_prev, d_own, d_next = lax.optimization_barrier(
        (received, dq_row, d_prev, d_own, d_next)
    )
    from_after = shifted(d_prev, "seq", -1)
    from_before = shifted(d_next, "seq", 1)

    grid_rows = tokens * devices // COLS
    arrival = jnp.arange(tokens, dtype=jnp.int32)
    col_block = ((arrival % GROUP_COLS) * grid_rows + arrival // GROUP_COLS) // BLOCK
    local_strided = strided_lists - position * block_count
    listed = sum(
        (col_block == number)[:, None] * local_strided[number][None, :]
        for number in range(block_count)
    )
    col_keep = jnp.any(listed[:, :, None] == col_block[None, None, :], axis=1).astype(jnp.float32)
    col_grads = col_side(received, col_keep).reshape(3, devices, share, 1, COLS)
    half = COLS // 2
    early, late = col_grads[..., :half], col_grads[..., half:]

    early, late, from_after, from_before = lax.optimization_barrier(
        (early, late, from_after, from_before)
    )
    d_total = (d_own + from_before.astype(jnp.float32) + from_after.astype(jnp.float32)).astype(
        jnp.bfloat16
    )
    row_grads = jnp.concatenate([dq_row[None], d_total], axis=0)
    row_handed = shifted(row_grads, "pipe", -1)
    early = shifted(early, "pipe", -1)
    late = lax.all_to_all(late, "seq", split_axis=1, concat_axis=3, tiled=True)

    early, late = lax.optimization_barrier((early, late))
    early = lax.all_to_all(early, "seq", split_axis=1, concat_axis=3, tiled=True)
    late = shifted(late, "pipe", -1)
    col_handed = jnp.concatenate(
        [early.reshape(3, tokens, half), late.reshape(3, tokens, half)], axis=2
    )

    handed = jnp.concatenate([row_handed, col_handed], axis=2)
    return (handed[0][None], handed[1][None], handed[2][None])


def solution(mesh):
    in_specs = (
        P("pipe", "seq", None),
        P("pipe", "seq", None),
        P("pipe", "seq", None),
        P("pipe", "seq", None),
        P("seq", None),
        P("seq", None),
    )
    out_specs = (P("pipe", "seq", None), P("pipe", "seq", None), P("pipe", "seq", None))
    return jax.shard_map(body, mesh=mesh, in_specs=in_specs, out_specs=out_specs, check_vma=False)
```

```python
import jax
import jax.numpy as jnp
from jax import lax
from jax.experimental import pallas as pl
from jax.experimental.pallas import tpu as pltpu
from jax.sharding import PartitionSpec as P

HEADS_ROW = 8
HEADS_COL = 8
HEAD_DIM = 128
COLS = 1024
BLOCK = 128
REACH = 3
GROUP_COLS = 16


def shifted(value, axis, steps):
    count = lax.axis_size(axis)
    pairs = [(source, (source + steps) % count) for source in range(count)]
    return lax.ppermute(value, axis, pairs)


def chunk_grads(q, do, k, v, keep, scale):
    scores = lax.dot_general(q, k, (((1,), (1,)), ((), ())), preferred_element_type=jnp.float32)
    scores = jnp.where(keep, scores * scale, -jnp.inf)
    largest = jnp.max(scores, axis=1, keepdims=True)
    raised = jnp.exp(scores - largest)
    softmax = raised / jnp.sum(raised, axis=1, keepdims=True)
    softmax_low = softmax.astype(jnp.bfloat16)
    attended = jnp.dot(softmax_low, v, preferred_element_type=jnp.float32)
    row_delta = jnp.sum(do.astype(jnp.float32) * attended, axis=1, keepdims=True)
    grad_softmax = lax.dot_general(
        do, v, (((1,), (1,)), ((), ())), preferred_element_type=jnp.float32
    )
    grad_scores = (scale * softmax * (grad_softmax - row_delta)).astype(jnp.bfloat16)
    grad_q = jnp.dot(grad_scores, k, preferred_element_type=jnp.float32)
    grad_k = lax.dot_general(
        grad_scores, q, (((0,), (0,)), ((), ())), preferred_element_type=jnp.float32
    )
    grad_v = lax.dot_general(
        softmax_low, do, (((0,), (0,)), ((), ())), preferred_element_type=jnp.float32
    )
    return grad_q, grad_k, grad_v


def row_kernel(
    q_ref, do_ref, kp_ref, ko_ref, kn_ref, vp_ref, vo_ref, vn_ref, keep_ref,
    dq_ref, dprev_ref, down_ref, dnext_ref, kwin, vwin, dkwin, dvwin,
):
    tokens = q_ref.shape[0]
    span = (2 * REACH + 1) * BLOCK
    scale = HEAD_DIM ** (-0.5)
    kwin[0:tokens, :] = kp_ref[...]
    kwin[tokens:2 * tokens, :] = ko_ref[...]
    kwin[2 * tokens:3 * tokens, :] = kn_ref[...]
    vwin[0:tokens, :] = vp_ref[...]
    vwin[tokens:2 * tokens, :] = vo_ref[...]
    vwin[2 * tokens:3 * tokens, :] = vn_ref[...]
    dkwin[...] = jnp.zeros_like(dkwin)
    dvwin[...] = jnp.zeros_like(dvwin)
    for i in range(tokens // BLOCK):
        rows = slice(i * BLOCK, (i + 1) * BLOCK)
        keys = slice(i * BLOCK, i * BLOCK + span)
        keep = keep_ref[i:i + 1, :] > 0.5
        grad_q, grad_k, grad_v = chunk_grads(
            q_ref[rows, :], do_ref[rows, :], kwin[keys, :], vwin[keys, :], keep, scale
        )
        dq_ref[rows, :] = grad_q.astype(dq_ref.dtype)
        dkwin[keys, :] += grad_k
        dvwin[keys, :] += grad_v
    dprev_ref[0] = dkwin[0:tokens, :].astype(dprev_ref.dtype)
    dprev_ref[1] = dvwin[0:tokens, :].astype(dprev_ref.dtype)
    down_ref[0] = dkwin[tokens:2 * tokens, :]
    down_ref[1] = dvwin[tokens:2 * tokens, :]
    dnext_ref[0] = dkwin[2 * tokens:3 * tokens, :].astype(dnext_ref.dtype)
    dnext_ref[1] = dvwin[2 * tokens:3 * tokens, :].astype(dnext_ref.dtype)


def col_kernel(q_ref, k_ref, v_ref, do_ref, keep_ref, out_ref):
    scale = HEAD_DIM ** (-0.5)
    keep = keep_ref[...] > 0.5
    grad_q, grad_k, grad_v = chunk_grads(
        q_ref[0], do_ref[0], k_ref[0], v_ref[0], keep, scale
    )
    out_ref[0] = grad_q.astype(out_ref.dtype)
    out_ref[1] = grad_k.astype(out_ref.dtype)
    out_ref[2] = grad_v.astype(out_ref.dtype)


def row_side(query_now, key_now, value_now, grad_now, near_before, near_after, keep):
    tokens = query_now.shape[0]
    span = (2 * REACH + 1) * BLOCK
    head_block = lambda h: (0, h)
    stacked_block = lambda part: pl.BlockSpec((None, tokens, HEAD_DIM), lambda h: (part, 0, h))
    plain = pl.BlockSpec((tokens, HEAD_DIM), head_block)
    pair_out = pl.BlockSpec((2, tokens, HEAD_DIM), lambda h: (0, 0, h))
    return pl.pallas_call(
        row_kernel,
        grid=(HEADS_ROW,),
        in_specs=[
            plain, plain,
            stacked_block(0), plain, stacked_block(0),
            stacked_block(1), plain, stacked_block(1),
            pl.BlockSpec(keep.shape, lambda h: (0, 0)),
        ],
        out_specs=[plain, pair_out, pair_out, pair_out],
        out_shape=[
            jax.ShapeDtypeStruct((tokens, HEADS_ROW * HEAD_DIM), jnp.bfloat16),
            jax.ShapeDtypeStruct((2, tokens, HEADS_ROW * HEAD_DIM), jnp.bfloat16),
            jax.ShapeDtypeStruct((2, tokens, HEADS_ROW * HEAD_DIM), jnp.float32),
            jax.ShapeDtypeStruct((2, tokens, HEADS_ROW * HEAD_DIM), jnp.bfloat16),
        ],
        scratch_shapes=[
            pltpu.VMEM((3 * tokens, HEAD_DIM), jnp.bfloat16),
            pltpu.VMEM((3 * tokens, HEAD_DIM), jnp.bfloat16),
            pltpu.VMEM((3 * tokens, HEAD_DIM), jnp.float32),
            pltpu.VMEM((3 * tokens, HEAD_DIM), jnp.float32),
        ],
    )(
        query_now, grad_now,
        near_before, key_now, near_after,
        near_before, value_now, near_after,
        keep,
    )


def col_side(received, keep):
    tokens = received.shape[1]
    part_block = lambda part: pl.BlockSpec((1, tokens, HEAD_DIM), lambda h: (part, 0, h))
    return pl.pallas_call(
        col_kernel,
        grid=(HEADS_COL,),
        in_specs=[
            part_block(0), part_block(1), part_block(2), part_block(3),
            pl.BlockSpec(keep.shape, lambda h: (0, 0)),
        ],
        out_specs=pl.BlockSpec((3, tokens, HEAD_DIM), lambda h: (0, 0, h)),
        out_shape=jax.ShapeDtypeStruct((3, tokens, HEADS_COL * HEAD_DIM), jnp.bfloat16),
    )(received, received, received, received, keep)


def body(query_act, key_act, value_act, out_grad, local_lists, strided_lists):
    devices = lax.axis_size("seq")
    position = lax.axis_index("seq")
    query_now = query_act[0]
    key_now = key_act[0]
    value_now = value_act[0]
    grad_now = out_grad[0]
    tokens = query_now.shape[0]
    block_count = tokens // BLOCK
    total_blocks = block_count * devices
    row_width = HEADS_ROW * HEAD_DIM
    share = tokens // devices

    near = jnp.stack([key_now[:, :row_width], value_now[:, :row_width]])
    near_before = shifted(near, "seq", 1)
    near_after = shifted(near, "seq", -1)
    sent = jnp.stack([item[:, row_width:] for item in (query_now, key_now, value_now, grad_now)])

    sent = sent.reshape(4, share, devices, COLS)
    sent, near_before, near_after = lax.optimization_barrier((sent, near_before, near_after))
    received = lax.all_to_all(
        sent, "seq", split_axis=2, concat_axis=1, tiled=True
    ).reshape(4, tokens, COLS)

    own_blocks = position * block_count + jnp.arange(block_count, dtype=jnp.int32)
    offsets = jnp.arange(-REACH, REACH + 1, dtype=jnp.int32)
    wanted = (own_blocks[:, None] + offsets[None, :]) % total_blocks
    row_allowed = jnp.any(wanted[:, :, None] == local_lists[:, None, :], axis=2)
    row_keep = jnp.repeat(row_allowed.astype(jnp.float32), BLOCK, axis=1)

    dq_row, d_prev, d_own, d_next = row_side(
        query_now, key_now, value_now, grad_now, near_before, near_after, row_keep
    )

    received, dq_row, d_prev, d_own, d_next = lax.optimization_barrier(
        (received, dq_row, d_prev, d_own, d_next)
    )
    from_after = shifted(d_prev, "seq", -1)
    from_before = shifted(d_next, "seq", 1)

    grid_rows = tokens * devices // COLS
    arrival = jnp.arange(tokens, dtype=jnp.int32)
    col_block = ((arrival % GROUP_COLS) * grid_rows + arrival // GROUP_COLS) // BLOCK
    local_strided = strided_lists - position * block_count
    listed = sum(
        (col_block == number)[:, None] * local_strided[number][None, :]
        for number in range(block_count)
    )
    col_keep = jnp.any(listed[:, :, None] == col_block[None, None, :], axis=1).astype(jnp.float32)
    col_grads = col_side(received, col_keep).reshape(3, devices, share, 1, COLS)
    half = COLS // 2
    early, late = col_grads[..., :half], col_grads[..., half:]

    early, late, from_after, from_before = lax.optimization_barrier(
        (early, late, from_after, from_before)
    )
    d_total = (d_own + from_before.astype(jnp.float32) + from_after.astype(jnp.float32)).astype(
        jnp.bfloat16
    )
    row_grads = jnp.concatenate([dq_row[None], d_total], axis=0)
    row_handed = shifted(row_grads, "pipe", -1)
    early = shifted(early, "pipe", -1)
    late = lax.all_to_all(late, "seq", split_axis=1, concat_axis=3, tiled=True)

    early, late = lax.optimization_barrier((early, late))
    early = lax.all_to_all(early, "seq", split_axis=1, concat_axis=3, tiled=True)
    late = shifted(late, "pipe", -1)
    early = early.reshape(3, tokens, half)
    late = late.reshape(3, tokens, half)
    return tuple(
        jnp.concatenate([row_handed[kind], early[kind], late[kind]], axis=1)[None]
        for kind in range(3)
    )


def solution(mesh):
    in_specs = (
        P("pipe", "seq", None),
        P("pipe", "seq", None),
        P("pipe", "seq", None),
        P("pipe", "seq", None),
        P("seq", None),
        P("seq", None),
    )
    out_specs = (P("pipe", "seq", None), P("pipe", "seq", None), P("pipe", "seq", None))
    return jax.shard_map(body, mesh=mesh, in_specs=in_specs, out_specs=out_specs, check_vma=False)
```

```python
import jax
import jax.numpy as jnp
from jax import lax
from jax.experimental import pallas as pl
from jax.experimental.pallas import tpu as pltpu
from jax.sharding import PartitionSpec as P

HEADS_ROW = 8
HEADS_COL = 8
HEAD_DIM = 128
COLS = 1024
BLOCK = 128
REACH = 3
GROUP_COLS = 16


def shifted(value, axis, steps):
    count = lax.axis_size(axis)
    pairs = [(source, (source + steps) % count) for source in range(count)]
    return lax.ppermute(value, axis, pairs)


def chunk_grads(q, do, k, v, keep, scale):
    scores = lax.dot_general(q, k, (((1,), (1,)), ((), ())), preferred_element_type=jnp.float32)
    scores = jnp.where(keep, scores * scale, -jnp.inf)
    largest = jnp.max(scores, axis=1, keepdims=True)
    raised = jnp.exp(scores - largest)
    softmax = raised / jnp.sum(raised, axis=1, keepdims=True)
    softmax_low = softmax.astype(jnp.bfloat16)
    attended = jnp.dot(softmax_low, v, preferred_element_type=jnp.float32)
    row_delta = jnp.sum(do.astype(jnp.float32) * attended, axis=1, keepdims=True)
    grad_softmax = lax.dot_general(
        do, v, (((1,), (1,)), ((), ())), preferred_element_type=jnp.float32
    )
    grad_scores = (scale * softmax * (grad_softmax - row_delta)).astype(jnp.bfloat16)
    grad_q = jnp.dot(grad_scores, k, preferred_element_type=jnp.float32)
    grad_k = lax.dot_general(
        grad_scores, q, (((0,), (0,)), ((), ())), preferred_element_type=jnp.float32
    )
    grad_v = lax.dot_general(
        softmax_low, do, (((0,), (0,)), ((), ())), preferred_element_type=jnp.float32
    )
    return grad_q, grad_k, grad_v


def row_kernel(
    q_ref, do_ref, kp_ref, ko_ref, kn_ref, vp_ref, vo_ref, vn_ref, keep_ref,
    dq_ref, dprev_ref, down_ref, dnext_ref, kwin, vwin, dkwin, dvwin,
):
    tokens = q_ref.shape[0]
    span = (2 * REACH + 1) * BLOCK
    scale = HEAD_DIM ** (-0.5)
    kwin[0:tokens, :] = kp_ref[...]
    kwin[tokens:2 * tokens, :] = ko_ref[...]
    kwin[2 * tokens:3 * tokens, :] = kn_ref[...]
    vwin[0:tokens, :] = vp_ref[...]
    vwin[tokens:2 * tokens, :] = vo_ref[...]
    vwin[2 * tokens:3 * tokens, :] = vn_ref[...]
    dkwin[...] = jnp.zeros_like(dkwin)
    dvwin[...] = jnp.zeros_like(dvwin)
    for i in range(tokens // BLOCK):
        rows = slice(i * BLOCK, (i + 1) * BLOCK)
        keys = slice(i * BLOCK, i * BLOCK + span)
        keep = keep_ref[i:i + 1, :] > 0.5
        grad_q, grad_k, grad_v = chunk_grads(
            q_ref[rows, :], do_ref[rows, :], kwin[keys, :], vwin[keys, :], keep, scale
        )
        dq_ref[rows, :] = grad_q.astype(dq_ref.dtype)
        dkwin[keys, :] += grad_k
        dvwin[keys, :] += grad_v
    dprev_ref[0] = dkwin[0:tokens, :].astype(dprev_ref.dtype)
    dprev_ref[1] = dvwin[0:tokens, :].astype(dprev_ref.dtype)
    down_ref[0] = dkwin[tokens:2 * tokens, :]
    down_ref[1] = dvwin[tokens:2 * tokens, :]
    dnext_ref[0] = dkwin[2 * tokens:3 * tokens, :].astype(dnext_ref.dtype)
    dnext_ref[1] = dvwin[2 * tokens:3 * tokens, :].astype(dnext_ref.dtype)


def col_kernel(q_ref, k_ref, v_ref, do_ref, keep_ref, out_ref):
    scale = HEAD_DIM ** (-0.5)
    keep = keep_ref[...] > 0.5
    grad_q, grad_k, grad_v = chunk_grads(
        q_ref[0], do_ref[0], k_ref[0], v_ref[0], keep, scale
    )
    out_ref[0] = grad_q.astype(out_ref.dtype)
    out_ref[1] = grad_k.astype(out_ref.dtype)
    out_ref[2] = grad_v.astype(out_ref.dtype)


def row_side(query_now, key_now, value_now, grad_now, near_before, near_after, keep):
    tokens = query_now.shape[0]
    span = (2 * REACH + 1) * BLOCK
    head_block = lambda h: (0, h)
    stacked_block = lambda part: pl.BlockSpec((None, tokens, HEAD_DIM), lambda h: (part, 0, h))
    plain = pl.BlockSpec((tokens, HEAD_DIM), head_block)
    pair_out = pl.BlockSpec((2, tokens, HEAD_DIM), lambda h: (0, 0, h))
    return pl.pallas_call(
        row_kernel,
        grid=(HEADS_ROW,),
        in_specs=[
            plain, plain,
            stacked_block(0), plain, stacked_block(0),
            stacked_block(1), plain, stacked_block(1),
            pl.BlockSpec(keep.shape, lambda h: (0, 0)),
        ],
        out_specs=[plain, pair_out, pair_out, pair_out],
        out_shape=[
            jax.ShapeDtypeStruct((tokens, HEADS_ROW * HEAD_DIM), jnp.bfloat16),
            jax.ShapeDtypeStruct((2, tokens, HEADS_ROW * HEAD_DIM), jnp.bfloat16),
            jax.ShapeDtypeStruct((2, tokens, HEADS_ROW * HEAD_DIM), jnp.float32),
            jax.ShapeDtypeStruct((2, tokens, HEADS_ROW * HEAD_DIM), jnp.bfloat16),
        ],
        scratch_shapes=[
            pltpu.VMEM((3 * tokens, HEAD_DIM), jnp.bfloat16),
            pltpu.VMEM((3 * tokens, HEAD_DIM), jnp.bfloat16),
            pltpu.VMEM((3 * tokens, HEAD_DIM), jnp.float32),
            pltpu.VMEM((3 * tokens, HEAD_DIM), jnp.float32),
        ],
    )(
        query_now, grad_now,
        near_before, key_now, near_after,
        near_before, value_now, near_after,
        keep,
    )


def col_side(received, keep):
    tokens = received.shape[1]
    part_block = lambda part: pl.BlockSpec((1, tokens, HEAD_DIM), lambda h: (part, 0, h))
    return pl.pallas_call(
        col_kernel,
        grid=(HEADS_COL,),
        in_specs=[
            part_block(0), part_block(1), part_block(2), part_block(3),
            pl.BlockSpec(keep.shape, lambda h: (0, 0)),
        ],
        out_specs=pl.BlockSpec((3, tokens, HEAD_DIM), lambda h: (0, 0, h)),
        out_shape=jax.ShapeDtypeStruct((3, tokens, HEADS_COL * HEAD_DIM), jnp.bfloat16),
    )(received, received, received, received, keep)


def body(query_act, key_act, value_act, out_grad, local_lists, strided_lists):
    devices = lax.axis_size("seq")
    position = lax.axis_index("seq")
    query_now = query_act[0]
    key_now = key_act[0]
    value_now = value_act[0]
    grad_now = out_grad[0]
    tokens = query_now.shape[0]
    block_count = tokens // BLOCK
    total_blocks = block_count * devices
    row_width = HEADS_ROW * HEAD_DIM
    share = tokens // devices

    near = jnp.stack([key_now[:, :row_width], value_now[:, :row_width]])
    near_before = shifted(near, "seq", 1)
    near_after = shifted(near, "seq", -1)
    sent = jnp.stack([item[:, row_width:] for item in (query_now, key_now, value_now, grad_now)])

    sent = sent.reshape(4, share, devices, COLS)
    sent, near_before, near_after = lax.optimization_barrier((sent, near_before, near_after))
    received = lax.all_to_all(
        sent, "seq", split_axis=2, concat_axis=1, tiled=True
    ).reshape(4, tokens, COLS)

    own_blocks = position * block_count + jnp.arange(block_count, dtype=jnp.int32)
    offsets = jnp.arange(-REACH, REACH + 1, dtype=jnp.int32)
    wanted = (own_blocks[:, None] + offsets[None, :]) % total_blocks
    row_allowed = jnp.any(wanted[:, :, None] == local_lists[:, None, :], axis=2)
    row_keep = jnp.repeat(row_allowed.astype(jnp.float32), BLOCK, axis=1)

    dq_row, d_prev, d_own, d_next = row_side(
        query_now, key_now, value_now, grad_now, near_before, near_after, row_keep
    )

    received, dq_row, d_prev, d_own, d_next = lax.optimization_barrier(
        (received, dq_row, d_prev, d_own, d_next)
    )
    from_after = shifted(d_prev, "seq", -1)
    from_before = shifted(d_next, "seq", 1)

    grid_rows = tokens * devices // COLS
    arrival = jnp.arange(tokens, dtype=jnp.int32)
    col_block = ((arrival % GROUP_COLS) * grid_rows + arrival // GROUP_COLS) // BLOCK
    local_strided = strided_lists - position * block_count
    listed = sum(
        (col_block == number)[:, None] * local_strided[number][None, :]
        for number in range(block_count)
    )
    col_keep = jnp.any(listed[:, :, None] == col_block[None, None, :], axis=1).astype(jnp.float32)
    col_grads = col_side(received, col_keep).reshape(3, devices, share, 1, COLS)
    half = COLS // 2
    early, late = col_grads[..., :half], col_grads[..., half:]

    early, late, from_after, from_before = lax.optimization_barrier(
        (early, late, from_after, from_before)
    )
    d_total = (d_own + from_before.astype(jnp.float32) + from_after.astype(jnp.float32)).astype(
        jnp.bfloat16
    )
    row_grads = jnp.concatenate([dq_row[None], d_total], axis=0)
    row_handed = shifted(row_grads, "pipe", -1)
    early = shifted(early, "pipe", -1)
    late = lax.all_to_all(late, "seq", split_axis=1, concat_axis=3, tiled=True)

    early = lax.all_to_all(early, "seq", split_axis=1, concat_axis=3, tiled=True)
    late = shifted(late, "pipe", -1)
    col_handed = jnp.concatenate(
        [early.reshape(3, tokens, half), late.reshape(3, tokens, half)], axis=2
    )

    handed = jnp.concatenate([row_handed, col_handed], axis=2)
    return (handed[0][None], handed[1][None], handed[2][None])


def solution(mesh):
    in_specs = (
        P("pipe", "seq", None),
        P("pipe", "seq", None),
        P("pipe", "seq", None),
        P("pipe", "seq", None),
        P("seq", None),
        P("seq", None),
    )
    out_specs = (P("pipe", "seq", None), P("pipe", "seq", None), P("pipe", "seq", None))
    return jax.shard_map(body, mesh=mesh, in_specs=in_specs, out_specs=out_specs, check_vma=False)
```
